256 devices in a mesh: section: 4 (over y), expert: 64 (over x, z, core).
Axes of the slice: x: 4, y: 4, z: 8, core: 2. Of those that a mesh axis runs over, the one named last changes fastest.
Arguments:
- tokens: bfloat16 [1024, 4096], P('expert', 'section'), may hold values from -6 to 6
- cotangent: bfloat16 [1024, 4096], P('expert', 'section'), may hold values from -6 to 6
- routes: int32 [1024, 2], P('expert'), may hold values from 0 to 7, all different within a row; in each aligned block of 16 rows (0 to 15, 16 to 31, ...) at most 6 rows name the same one
- w_router: bfloat16 [4096, 8], P('section'), may hold values from -0.09375 to 0.09375
- w_gate: bfloat16 [64, 4096, 1024], P('expert', None, 'section'), may hold values from -0.09375 to 0.09375
- w_up: bfloat16 [64, 4096, 1024], P('expert', None, 'section'), may hold values from -0.09375 to 0.09375
- w_down: bfloat16 [64, 1024, 4096], P('expert', 'section'), may hold values from -0.0625 to 0.0625
Outputs:
- mixed: bfloat16 [1024, 4096], P('expert', 'section')
- grad_tokens: bfloat16 [1024, 4096], P('expert', 'section')
- grad_router: float32 [4096, 8], P('section')
- grad_gate: bfloat16 [64, 4096, 1024], P('expert', None, 'section')
- grad_up: bfloat16 [64, 4096, 1024], P('expert', None, 'section')
- grad_down: bfloat16 [64, 1024, 4096], P('expert', 'section')
The draws below stay inside these ranges and needn't reach their ends.
Inputs may be any that keep to these rules, and one draw needn't show every extreme that they name: `routes`: each token names two different experts. Within each aligned block of 16 tokens no expert is named by more than 6 tokens, and in every draw some block has an expert named by exactly 6 tokens.
All inputs are finite; a program needn't handle non-finite values.
Results may differ from the reference program's by a relative error of at most 0.023.
Values may be sent and summed in bfloat16 or wider, within the bound.
No kernel may reach another device: no remote copies, remote signals or barrier semaphores. Data moves between devices by JAX's collectives and lax.ppermute only.
A program may use at most 128 MiB of HBM per device.

```python
import math
import jax
import jax.numpy as jnp
import numpy as np
from jax import lax

D = 4096
E = 8
FF = 8192
TOK_DEV = 16
CAP = 6
SLICE = 1024
TOKENS = 1024
N_SECTION = 4
N_EXPERT = 64


def shard_levels(rng, dims, pieces, low, largest):
    def one(dim, blocks):
        draws = jax.random.uniform(jax.random.fold_in(jax.random.fold_in(rng, 6), dim), (blocks,), jnp.float32, low / len(pieces), largest / len(pieces))
        return jnp.repeat(jnp.exp(draws), dims[dim] // blocks).reshape((-1,) + (1,) * (len(dims) - dim - 1))

    level = one(*pieces[0])
    for cut in pieces[1:]:
        level = level * one(*cut)
    return level


def assign_block(rng, own, number, rows, count, top, most, lean):
    order = jax.random.permutation(rng, count)
    packed, usual = shares(count, rows * top, most, lean, True), shares(count, rows * top, most, lean, False)
    places = jnp.arange(count)

    def named(tallies, rotation):
        used = int((tallies > 0).sum())
        fixed = max(1, used // 4)
        shifted = fixed + (places - fixed + rotation * (used - fixed)) % max(1, count - fixed)
        return jnp.zeros((count,), jnp.int32).at[order[jnp.where(places < fixed, places, shifted)]].set(jnp.asarray(tallies, jnp.int32))

    tallies = jnp.where(number % 4 == 0, named(packed, number // 4), named(usual, number - number // 4 - 1))
    mixed = jax.random.permutation(jax.random.fold_in(own, 3), count)
    donor, taker = mixed[0:count // 2 * 2:2], mixed[1:count // 2 * 2:2]
    slack = jnp.minimum(tallies[donor] - 1, most - tallies[taker]) // 2
    slack = jnp.where((donor == order[0]) | (taker == order[0]) | (tallies[taker] == 0), 0, jnp.maximum(slack, 0))
    shifted = jax.random.randint(jax.random.fold_in(own, 4), (count // 2,), 0, 1 << 20) % (slack + 1)
    tallies = tallies.at[donor].add(-shifted).at[taker].add(shifted)
    labels = jnp.searchsorted(jnp.cumsum(tallies), jnp.arange(rows * top), side="right").astype(jnp.int32)
    listing = labels.reshape(top, rows).T
    listing = listing[jax.random.permutation(jax.random.fold_in(own, 1), rows)]
    rotation = jax.random.randint(jax.random.fold_in(own, 2), (rows, 1), 0, top)
    return jnp.take_along_axis(listing, (jnp.arange(top)[None, :] + rotation) % top, axis=1)


def shares(amount, total, limit, lean, full):
    weights = [(1 << 20) // math.isqrt(grade ** lean) + 1 for grade in range(1, amount + 1)]
    largest = limit if full else min(limit, max(-(-total // amount), total * weights[0] // sum(weights)))
    least = 1 if total - largest >= amount - 1 else 0
    counts, spare = [largest] + [least] * (amount - 1), total - largest - least * (amount - 1)
    while spare > 0:
        candidates = [i for i in range(1, amount) if counts[i] < largest] or [i for i in range(1, amount) if counts[i] < limit]
        whole, remaining = sum([weights[i] for i in candidates]), spare
        for i in candidates:
            addition = min(limit - counts[i], max(1, remaining * weights[i] // whole), spare)
            counts[i] = counts[i] + addition
            spare = spare - addition
    return np.array(counts)


def normal_values(key, shape, width, reach, cuts=(), kind=jnp.bfloat16):
    result = jax.random.normal(key, shape, jnp.float32) * width
    if len(cuts) > 0:
        result = shard_levels(key, shape, cuts, -0.22, 0.18) * result
    return jnp.clip(result, min=-reach, max=reach).astype(kind)


def setup_inputs(seed: int = 0) -> dict:
    key_list = jax.random.split(jax.random.key(seed), 8)
    tokens = normal_values(key_list[0], (TOKENS, D), 1.0, 6.0, ((0, 64), (1, 4)))
    cotangent = normal_values(key_list[1], (TOKENS, D), 1.0, 6.0, ((0, 64), (1, 4)))
    routes_keys = jax.random.split(jax.random.fold_in(key_list[2], 1), TOKENS // TOK_DEV)
    routes_turns = jax.random.permutation(jax.random.fold_in(key_list[2], 3), TOKENS // TOK_DEV)
    routes = jax.vmap(lambda own, number: assign_block(jax.random.fold_in(key_list[2], 2), own, number, TOK_DEV, E, 2, CAP, 2))(routes_keys, routes_turns).reshape((TOKENS, 2))
    w_router = normal_values(key_list[3], (D, E), D ** -0.5, 0.09375, ((0, 4),))
    w_gate = normal_values(key_list[4], (N_EXPERT, D, SLICE), D ** -0.5, 0.09375, ((0, 64), (2, 4)))
    w_up = normal_values(key_list[5], (N_EXPERT, D, SLICE), D ** -0.5, 0.09375, ((0, 64), (2, 4)))
    w_down = normal_values(key_list[6], (N_EXPERT, SLICE, D), FF ** -0.5, 0.0625, ((0, 64), (1, 4)))
    return dict(tokens=tokens, cotangent=cotangent, routes=routes, w_router=w_router, w_gate=w_gate, w_up=w_up, w_down=w_down)


def reference(tokens, cotangent, routes, w_router, w_gate, w_up, w_down):
    groups = N_EXPERT // E
    unit_count = SLICE // N_SECTION
    slices = groups * N_SECTION
    row_count = N_EXPERT * CAP
    highest = lax.Precision.HIGHEST
    logits = jnp.dot(tokens, w_router, preferred_element_type=jnp.float32)
    route_hot = routes[:, :, None] == jnp.arange(E, dtype=jnp.int32)[None, None, :]
    chosen = jnp.sum(jnp.where(route_hot, logits[:, None, :], jnp.zeros((), jnp.float32)), axis=2)
    gate_first = 1.0 / (1.0 + jnp.exp(chosen[:, 1] - chosen[:, 0]))
    gate_second = 1.0 / (1.0 + jnp.exp(chosen[:, 0] - chosen[:, 1]))
    gates = jnp.stack([gate_first, gate_second], axis=1)
    counts_block = route_hot.astype(jnp.int32).reshape(N_EXPERT, 2 * TOK_DEV, E)
    earlier = jnp.cumsum(counts_block, axis=1) - counts_block
    position = jnp.sum(earlier * counts_block, axis=2).reshape(TOKENS, 2)
    source_block = (jnp.arange(TOKENS, dtype=jnp.int32) // TOK_DEV).astype(jnp.int32)
    slot_row = (source_block[:, None] * CAP + position).astype(jnp.int32)
    assign_id = jnp.arange(2 * TOKENS, dtype=jnp.int32).reshape(TOKENS, 2)
    slot_assign = jnp.zeros((E, row_count), jnp.int32).at[routes, slot_row].set(assign_id)
    slot_valid = jnp.zeros((E, row_count), jnp.int32).at[routes, slot_row].set(jnp.ones((TOKENS, 2), jnp.int32))
    scaled = (gates[:, :, None] * cotangent.astype(jnp.float32)[:, None, :]).astype(jnp.bfloat16).reshape(2 * TOKENS, D)
    doubled = jnp.repeat(tokens, 2, axis=0)
    zero_bf = jnp.zeros((), jnp.bfloat16)

    def expert_pass(expert_id):
        token_slot = slot_assign[expert_id]
        row_mask = slot_valid[expert_id][:, None] > 0
        x_rows = jnp.where(row_mask, doubled[token_slot], zero_bf)
        dy_rows = jnp.where(row_mask, scaled[token_slot], zero_bf)
        start = (expert_id * groups).astype(jnp.int32)
        gate_local = lax.dynamic_slice_in_dim(w_gate, start, groups, 0)
        up_local = lax.dynamic_slice_in_dim(w_up, start, groups, 0)
        down_local = lax.dynamic_slice_in_dim(w_down, start, groups, 0)
        down_flat = down_local.reshape(FF, D)
        x_float = x_rows.astype(jnp.float32)
        pre_gate = jnp.einsum("rd,gdf->rgf", x_float, gate_local.astype(jnp.float32), precision=highest).reshape(row_count, FF)
        pre_up = jnp.einsum("rd,gdf->rgf", x_float, up_local.astype(jnp.float32), precision=highest).reshape(row_count, FF)
        sigmoid_gate = jax.nn.sigmoid(pre_gate)
        activated = pre_gate * sigmoid_gate
        hidden = (activated * pre_up).astype(jnp.bfloat16)
        d_hidden = jnp.dot(dy_rows, down_flat.T, preferred_element_type=jnp.float32)
        grad_down_e = jnp.dot(hidden.T, dy_rows, preferred_element_type=jnp.float32).astype(jnp.bfloat16).reshape(groups, SLICE, D)
        d_pre_gate = (d_hidden * pre_up * sigmoid_gate * (1.0 + pre_gate * (1.0 - sigmoid_gate))).astype(jnp.bfloat16)
        d_pre_up = (d_hidden * activated).astype(jnp.bfloat16)
        grad_gate_e = jnp.einsum("rd,rgf->gdf", x_float, d_pre_gate.astype(jnp.float32).reshape(row_count, groups, SLICE), precision=highest).astype(jnp.bfloat16)
        grad_up_e = jnp.einsum("rd,rgf->gdf", x_float, d_pre_up.astype(jnp.float32).reshape(row_count, groups, SLICE), precision=highest).astype(jnp.bfloat16)

        def add_piece(carry, piece_id):
            total_out, total_dx = carry
            group_id = (piece_id // N_SECTION).astype(jnp.int32)
            section_id = (piece_id % N_SECTION).astype(jnp.int32)
            column = (piece_id * unit_count).astype(jnp.int32)
            zero_index = jnp.zeros((), jnp.int32)
            hidden_piece = lax.dynamic_slice_in_dim(hidden, column, unit_count, 1)
            down_piece = lax.dynamic_slice_in_dim(down_flat, column, unit_count, 0)
            part_out = jnp.dot(hidden_piece, down_piece, preferred_element_type=jnp.float32).astype(jnp.bfloat16)
            part_out = lax.optimization_barrier(part_out).astype(jnp.float32)
            inner = (section_id * unit_count).astype(jnp.int32)
            gate_piece = lax.dynamic_slice(gate_local, (group_id, zero_index, inner), (1, D, unit_count))[0]
            up_piece = lax.dynamic_slice(up_local, (group_id, zero_index, inner), (1, D, unit_count))[0]
            dg_piece = lax.dynamic_slice_in_dim(d_pre_gate, column, unit_count, 1)
            du_piece = lax.dynamic_slice_in_dim(d_pre_up, column, unit_count, 1)
            part_dx = jnp.dot(dg_piece, gate_piece.T, preferred_element_type=jnp.float32) + jnp.dot(du_piece, up_piece.T, preferred_element_type=jnp.float32)
            part_dx = lax.optimization_barrier(part_dx.astype(jnp.bfloat16)).astype(jnp.float32)
            return (total_out + part_out, total_dx + part_dx), None

        empty = jnp.zeros((row_count, D), jnp.float32)
        (expert_out, expert_dx), unused = lax.scan(add_piece, (empty, empty), jnp.arange(slices, dtype=jnp.int32))
        return expert_out, expert_dx, grad_gate_e, grad_up_e, grad_down_e

    expert_out, expert_dx, grad_gate, grad_up, grad_down = lax.map(expert_pass, jnp.arange(E, dtype=jnp.int32))
    out_assign = expert_out[routes, slot_row]
    mixed = (gates[:, 0:1] * out_assign[:, 0] + gates[:, 1:2] * out_assign[:, 1]).astype(jnp.bfloat16)
    cot_float = cotangent.astype(jnp.float32)
    gate_inner = jnp.sum(cot_float[:, None, :] * out_assign, axis=2)
    d_first = gate_first * gate_second * (gate_inner[:, 0] - gate_inner[:, 1])
    zero_f = jnp.zeros((), jnp.float32)
    d_logits = jnp.where(route_hot[:, 0, :], d_first[:, None], zero_f) - jnp.where(route_hot[:, 1, :], d_first[:, None], zero_f)
    dx_assign = expert_dx[routes, slot_row]
    grad_tokens = (dx_assign[:, 0] + dx_assign[:, 1] + jnp.dot(d_logits, w_router.astype(jnp.float32).T, precision=highest)).astype(jnp.bfloat16)
    grad_router = jnp.dot(tokens.astype(jnp.float32).T, d_logits, precision=highest)
    return (mixed, grad_tokens, grad_router, grad_gate.reshape(N_EXPERT, D, SLICE), grad_up.reshape(N_EXPERT, D, SLICE), grad_down.reshape(N_EXPERT, SLICE, D))
```

```python
import jax
import jax.numpy as jnp
import numpy as np
from jax import lax
from jax.sharding import Mesh
from jax.sharding import PartitionSpec as P

CAP = 6
LANES = 128
EXPERT_AXES = ("ex", "ez", "ec")


def expert_size():
    size = 1
    for name in EXPERT_AXES:
        size = size * lax.axis_size(name)
    return size


def per_device(tokens, cotangent, routes, w_router, w_gate, w_up, w_down):
    highest = lax.Precision.HIGHEST
    experts = w_router.shape[1]
    groups = expert_size() // experts
    capacity = CAP
    tok_count, width = tokens.shape
    n_section = lax.axis_size("section")
    slot_total = experts * capacity
    partial_logits = jnp.dot(tokens, w_router, preferred_element_type=jnp.float32)
    logits = lax.psum(partial_logits, "section")
    route_hot = routes[:, :, None] == jnp.arange(experts, dtype=jnp.int32)[None, None, :]
    zero_f = jnp.zeros((), jnp.float32)
    chosen = jnp.sum(jnp.where(route_hot, logits[:, None, :], zero_f), axis=2)
    gate_first = 1.0 / (1.0 + jnp.exp(chosen[:, 1] - chosen[:, 0]))
    gate_second = 1.0 / (1.0 + jnp.exp(chosen[:, 0] - chosen[:, 1]))
    counts_flat = route_hot.astype(jnp.int32).reshape(2 * tok_count, experts)
    earlier = jnp.cumsum(counts_flat, axis=0) - counts_flat
    position = jnp.sum(earlier * counts_flat, axis=1).reshape(tok_count, 2)
    slot_row = routes * capacity + position
    slot_ids = jnp.arange(slot_total, dtype=jnp.int32)[None, :]
    pick_first = slot_row[:, 0:1] == slot_ids
    pick_second = slot_row[:, 1:2] == slot_ids
    pick_both = (pick_first | pick_second).astype(jnp.bfloat16)
    x_source = jnp.einsum(
        "ts,td->sd", pick_both, tokens, preferred_element_type=jnp.float32
    ).astype(jnp.bfloat16)
    cot_float = cotangent.astype(jnp.float32)
    scaled_first = (gate_first[:, None] * cot_float).astype(jnp.bfloat16)
    scaled_second = (gate_second[:, None] * cot_float).astype(jnp.bfloat16)
    dy_source = jnp.einsum(
        "ts,td->sd",
        pick_first.astype(jnp.bfloat16),
        scaled_first,
        preferred_element_type=jnp.float32,
    )
    dy_source = dy_source + jnp.einsum(
        "ts,td->sd",
        pick_second.astype(jnp.bfloat16),
        scaled_second,
        preferred_element_type=jnp.float32,
    )
    dy_source = dy_source.astype(jnp.bfloat16)
    both_source = jnp.stack(
        [x_source.reshape(experts, capacity * width), dy_source.reshape(experts, capacity * width)],
        axis=1,
    )
    block_rows = 2 * capacity * width // LANES
    sent = jnp.broadcast_to(
        both_source.reshape(experts, 1, block_rows, LANES), (experts, groups, block_rows, LANES)
    ).reshape(experts * groups, block_rows, LANES)
    received = lax.all_to_all(sent, EXPERT_AXES, 0, 0, tiled=True)
    row_total = received.shape[0] * capacity
    received = received.reshape(-1, 2, capacity, width).transpose(1, 0, 2, 3)
    received = received.reshape(2, row_total, width)
    gathered = lax.all_gather(received, "section", axis=2, tiled=True)
    x_rows = gathered[0]
    dy_rows = gathered[1]
    gate_local = w_gate[0]
    up_local = w_up[0]
    down_local = w_down[0]
    pre_gate = jnp.dot(x_rows, gate_local, preferred_element_type=jnp.float32)
    pre_up = jnp.dot(x_rows, up_local, preferred_element_type=jnp.float32)
    sigmoid_gate = jax.nn.sigmoid(pre_gate)
    activated = pre_gate * sigmoid_gate
    hidden = (activated * pre_up).astype(jnp.bfloat16)
    d_hidden = jnp.einsum("pd,fd->pf", dy_rows, down_local, preferred_element_type=jnp.float32)
    grad_down = jnp.einsum("pf,pd->fd", hidden, dy_rows, preferred_element_type=jnp.float32).astype(
        jnp.bfloat16
    )
    d_pre_gate = (
        d_hidden * pre_up * sigmoid_gate * (1.0 + pre_gate * (1.0 - sigmoid_gate))
    ).astype(jnp.bfloat16)
    d_pre_up = (d_hidden * activated).astype(jnp.bfloat16)
    grad_gate = jnp.einsum(
        "pd,pf->df", x_rows, d_pre_gate, preferred_element_type=jnp.float32
    ).astype(jnp.bfloat16)
    grad_up = jnp.einsum("pd,pf->df", x_rows, d_pre_up, preferred_element_type=jnp.float32).astype(
        jnp.bfloat16
    )
    hid = gate_local.shape[1]
    down_blocks = down_local.reshape(hid, n_section, width)
    gate_blocks = gate_local.reshape(n_section, width, hid)
    up_blocks = up_local.reshape(n_section, width, hid)
    out_piece = jnp.einsum("pf,fsd->spd", hidden, down_blocks, preferred_element_type=jnp.float32)
    dx_piece = jnp.einsum("pf,sdf->spd", d_pre_gate, gate_blocks, preferred_element_type=jnp.float32)
    dx_piece = dx_piece + jnp.einsum(
        "pf,sdf->spd", d_pre_up, up_blocks, preferred_element_type=jnp.float32
    )
    pieces = jnp.stack([out_piece, dx_piece], axis=1).astype(jnp.bfloat16)
    pieces = pieces.reshape(n_section * 2 * pieces.shape[2], width)
    reduced = lax.psum_scatter(pieces, "section", scatter_dimension=0, tiled=True)
    n_dev = row_total // capacity
    back = reduced.reshape(2, n_dev, capacity, width).transpose(1, 0, 2, 3)
    back = back.reshape(n_dev, block_rows, LANES)
    returned = lax.all_to_all(back, EXPERT_AXES, 0, 0, tiled=True)
    returned = returned.reshape(experts, groups, 2, capacity, width).astype(jnp.float32)
    folded = jnp.sum(returned, axis=1)
    slot_out = folded[:, 0].reshape(slot_total, width)
    slot_dx = folded[:, 1].reshape(slot_total, width)
    first_float = pick_first.astype(jnp.float32)
    second_float = pick_second.astype(jnp.float32)
    out_first = jnp.dot(first_float, slot_out, precision=highest)
    out_second = jnp.dot(second_float, slot_out, precision=highest)
    mixed = (gate_first[:, None] * out_first + gate_second[:, None] * out_second).astype(
        jnp.bfloat16
    )
    local_inner = jnp.stack(
        [jnp.sum(cot_float * out_first, axis=1), jnp.sum(cot_float * out_second, axis=1)], axis=1
    )
    gate_inner = lax.psum(local_inner, "section")
    d_first = gate_first * gate_second * (gate_inner[:, 0] - gate_inner[:, 1])
    d_logits = jnp.where(route_hot[:, 0, :], d_first[:, None], zero_f) - jnp.where(
        route_hot[:, 1, :], d_first[:, None], zero_f
    )
    dx_expert = jnp.dot(first_float, slot_dx, precision=highest)
    dx_expert = dx_expert + jnp.dot(second_float, slot_dx, precision=highest)
    router_float = w_router.astype(jnp.float32)
    grad_tokens = (dx_expert + jnp.dot(d_logits, router_float.T, precision=highest)).astype(
        jnp.bfloat16
    )
    router_part = jnp.einsum(
        "te,tf->ef", d_logits, tokens.astype(jnp.float32), precision=highest
    )
    for name in reversed(EXPERT_AXES):
        router_part = lax.psum(router_part, name)
    grad_router = router_part.T
    return (mixed, grad_tokens, grad_router, grad_gate[None], grad_up[None], grad_down[None])


def expert_shape(devices):
    try:
        xs = sorted({d.coords[0] for d in devices.flat})
        zs = sorted({d.coords[2] for d in devices.flat})
        cores = sorted({d.core_on_chip for d in devices.flat})
        shape = (len(xs), len(zs), len(cores))
    except AttributeError:
        shape = (4, 8, 2)
    if int(np.prod(shape)) != devices.shape[1]:
        shape = (devices.shape[1] // 16, 8, 2)
    return shape


def solution(mesh):
    devices = mesh.devices
    fine = Mesh(
        devices.reshape((devices.shape[0],) + expert_shape(devices)),
        ("section",) + EXPERT_AXES,
    )
    ex = EXPERT_AXES
    in_specs = (
        P(ex, "section"),
        P(ex, "section"),
        P(ex, None),
        P("section", None),
        P(ex, None, "section"),
        P(ex, None, "section"),
        P(ex, "section", None),
    )
    out_specs = (
        P(ex, "section"),
        P(ex, "section"),
        P("section", None),
        P(ex, None, "section"),
        P(ex, None, "section"),
        P(ex, "section", None),
    )
    return jax.shard_map(
        per_device, mesh=fine, in_specs=in_specs, out_specs=out_specs, check_vma=False
    )
```

```python
import jax
import jax.numpy as jnp
import numpy as np
from jax import lax
from jax.sharding import Mesh
from jax.sharding import PartitionSpec as P

CAP = 6
LANES = 128
EXPERT_AXES = ("ex", "ez", "ec")


def expert_size():
    size = 1
    for name in EXPERT_AXES:
        size = size * lax.axis_size(name)
    return size


def per_device(tokens, cotangent, routes, w_router, w_gate, w_up, w_down):
    highest = lax.Precision.HIGHEST
    experts = w_router.shape[1]
    groups = expert_size() // experts
    capacity = CAP
    tok_count, width = tokens.shape
    n_section = lax.axis_size("section")
    slot_total = experts * capacity
    partial_logits = jnp.dot(tokens, w_router, preferred_element_type=jnp.float32)
    logits = lax.psum(partial_logits, "section")
    route_hot = routes[:, :, None] == jnp.arange(experts, dtype=jnp.int32)[None, None, :]
    zero_f = jnp.zeros((), jnp.float32)
    chosen = jnp.sum(jnp.where(route_hot, logits[:, None, :], zero_f), axis=2)
    gate_first = 1.0 / (1.0 + jnp.exp(chosen[:, 1] - chosen[:, 0]))
    gate_second = 1.0 / (1.0 + jnp.exp(chosen[:, 0] - chosen[:, 1]))
    counts_flat = route_hot.astype(jnp.int32).reshape(2 * tok_count, experts)
    earlier = jnp.cumsum(counts_flat, axis=0) - counts_flat
    position = jnp.sum(earlier * counts_flat, axis=1).reshape(tok_count, 2)
    slot_row = routes * capacity + position
    slot_ids = jnp.arange(slot_total, dtype=jnp.int32)[None, :]
    pick_first = slot_row[:, 0:1] == slot_ids
    pick_second = slot_row[:, 1:2] == slot_ids
    pick_both = (pick_first | pick_second).astype(jnp.bfloat16)
    x_source = jnp.einsum(
        "ts,td->sd", pick_both, tokens, preferred_element_type=jnp.float32
    ).astype(jnp.bfloat16)
    cot_float = cotangent.astype(jnp.float32)
    scaled_first = (gate_first[:, None] * cot_float).astype(jnp.bfloat16)
    scaled_second = (gate_second[:, None] * cot_float).astype(jnp.bfloat16)
    dy_source = jnp.einsum(
        "ts,td->sd",
        pick_first.astype(jnp.bfloat16),
        scaled_first,
        preferred_element_type=jnp.float32,
    )
    dy_source = dy_source + jnp.einsum(
        "ts,td->sd",
        pick_second.astype(jnp.bfloat16),
        scaled_second,
        preferred_element_type=jnp.float32,
    )
    dy_source = dy_source.astype(jnp.bfloat16)
    both_source = jnp.stack(
        [x_source.reshape(experts, capacity * width), dy_source.reshape(experts, capacity * width)],
        axis=1,
    )
    block_rows = 2 * capacity * width // LANES
    sent = jnp.broadcast_to(
        both_source.reshape(experts, 1, block_rows, LANES), (experts, groups, block_rows, LANES)
    ).reshape(experts * groups, block_rows, LANES)
    received = lax.all_to_all(sent, EXPERT_AXES, 0, 0, tiled=True)
    row_total = received.shape[0] * capacity
    half = block_rows // 2
    x_recv = received[:, :half].reshape(row_total, width)
    dy_recv = received[:, half:].reshape(row_total, width)
    x_rows = lax.all_gather(x_recv, "section", axis=1, tiled=True)
    dy_rows = lax.all_gather(dy_recv, "section", axis=1, tiled=True)
    gate_local = w_gate[0]
    up_local = w_up[0]
    down_local = w_down[0]
    pre_gate = jnp.dot(x_rows, gate_local, preferred_element_type=jnp.float32)
    pre_up = jnp.dot(x_rows, up_local, preferred_element_type=jnp.float32)
    sigmoid_gate = jax.nn.sigmoid(pre_gate)
    activated = pre_gate * sigmoid_gate
    hidden = (activated * pre_up).astype(jnp.bfloat16)
    d_hidden = jnp.einsum("pd,fd->pf", dy_rows, down_local, preferred_element_type=jnp.float32)
    grad_down = jnp.einsum("pf,pd->fd", hidden, dy_rows, preferred_element_type=jnp.float32).astype(
        jnp.bfloat16
    )
    d_pre_gate = (
        d_hidden * pre_up * sigmoid_gate * (1.0 + pre_gate * (1.0 - sigmoid_gate))
    ).astype(jnp.bfloat16)
    d_pre_up = (d_hidden * activated).astype(jnp.bfloat16)
    grad_gate = jnp.einsum(
        "pd,pf->df", x_rows, d_pre_gate, preferred_element_type=jnp.float32
    ).astype(jnp.bfloat16)
    grad_up = jnp.einsum("pd,pf->df", x_rows, d_pre_up, preferred_element_type=jnp.float32).astype(
        jnp.bfloat16
    )
    hid = gate_local.shape[1]
    down_blocks = down_local.reshape(hid, n_section, width)
    gate_blocks = gate_local.reshape(n_section, width, hid)
    up_blocks = up_local.reshape(n_section, width, hid)
    out_piece = jnp.einsum("pf,fsd->spd", hidden, down_blocks, preferred_element_type=jnp.float32)
    dx_piece = jnp.einsum("pf,sdf->spd", d_pre_gate, gate_blocks, preferred_element_type=jnp.float32)
    dx_piece = dx_piece + jnp.einsum(
        "pf,sdf->spd", d_pre_up, up_blocks, preferred_element_type=jnp.float32
    )
    out_red = lax.psum_scatter(
        out_piece.astype(jnp.bfloat16).reshape(n_section * row_total, width),
        "section",
        scatter_dimension=0,
        tiled=True,
    )
    dx_red = lax.psum_scatter(
        dx_piece.astype(jnp.bfloat16).reshape(n_section * row_total, width),
        "section",
        scatter_dimension=0,
        tiled=True,
    )
    n_dev = row_total // capacity
    back = jnp.stack(
        [out_red.reshape(n_dev, half, LANES), dx_red.reshape(n_dev, half, LANES)], axis=1
    ).reshape(n_dev, block_rows, LANES)
    returned = lax.all_to_all(back, EXPERT_AXES, 0, 0, tiled=True)
    returned = returned.reshape(experts, groups, 2, capacity, width).astype(jnp.float32)
    folded = jnp.sum(returned, axis=1)
    slot_out = folded[:, 0].reshape(slot_total, width)
    slot_dx = folded[:, 1].reshape(slot_total, width)
    first_float = pick_first.astype(jnp.float32)
    second_float = pick_second.astype(jnp.float32)
    out_first = jnp.dot(first_float, slot_out, precision=highest)
    out_second = jnp.dot(second_float, slot_out, precision=highest)
    mixed = (gate_first[:, None] * out_first + gate_second[:, None] * out_second).astype(
        jnp.bfloat16
    )
    local_inner = jnp.stack(
        [jnp.sum(cot_float * out_first, axis=1), jnp.sum(cot_float * out_second, axis=1)], axis=1
    )
    gate_inner = lax.psum(local_inner, "section")
    d_first = gate_first * gate_second * (gate_inner[:, 0] - gate_inner[:, 1])
    d_logits = jnp.where(route_hot[:, 0, :], d_first[:, None], zero_f) - jnp.where(
        route_hot[:, 1, :], d_first[:, None], zero_f
    )
    dx_expert = jnp.dot(first_float, slot_dx, precision=highest)
    dx_expert = dx_expert + jnp.dot(second_float, slot_dx, precision=highest)
    router_float = w_router.astype(jnp.float32)
    grad_tokens = (dx_expert + jnp.dot(d_logits, router_float.T, precision=highest)).astype(
        jnp.bfloat16
    )
    router_part = jnp.einsum(
        "te,tf->ef", d_logits, tokens.astype(jnp.float32), precision=highest
    )
    router_part = lax.psum(router_part, EXPERT_AXES[2])
    for name in (EXPERT_AXES[1], EXPERT_AXES[0]):
        router_part = jnp.sum(lax.all_gather(router_part, name, axis=0), axis=0)
    grad_router = router_part.T
    return (mixed, grad_tokens, grad_router, grad_gate[None], grad_up[None], grad_down[None])


def expert_shape(devices):
    try:
        xs = sorted({d.coords[0] for d in devices.flat})
        zs = sorted({d.coords[2] for d in devices.flat})
        cores = sorted({d.core_on_chip for d in devices.flat})
        shape = (len(xs), len(zs), len(cores))
    except AttributeError:
        shape = (4, 8, 2)
    if int(np.prod(shape)) != devices.shape[1]:
        shape = (devices.shape[1] // 16, 8, 2)
    return shape


def solution(mesh):
    devices = mesh.devices
    fine = Mesh(
        devices.reshape((devices.shape[0],) + expert_shape(devices)),
        ("section",) + EXPERT_AXES,
    )
    ex = EXPERT_AXES
    in_specs = (
        P(ex, "section"),
        P(ex, "section"),
        P(ex, None),
        P("section", None),
        P(ex, None, "section"),
        P(ex, None, "section"),
        P(ex, "section", None),
    )
    out_specs = (
        P(ex, "section"),
        P(ex, "section"),
        P("section", None),
        P(ex, None, "section"),
        P(ex, None, "section"),
        P(ex, "section", None),
    )
    return jax.shard_map(
        per_device, mesh=fine, in_specs=in_specs, out_specs=out_specs, check_vma=False
    )
```

```python
import jax
import jax.numpy as jnp
import numpy as np
from jax import lax
from jax.sharding import Mesh
from jax.sharding import PartitionSpec as P

CAP = 6
LANES = 128
EXPERT_AXES = ("ex", "ez", "ec")


def expert_size():
    size = 1
    for name in EXPERT_AXES:
        size = size * lax.axis_size(name)
    return size


def per_device(tokens, cotangent, routes, w_router, w_gate, w_up, w_down):
    highest = lax.Precision.HIGHEST
    experts = w_router.shape[1]
    groups = expert_size() // experts
    capacity = CAP
    tok_count, width = tokens.shape
    n_section = lax.axis_size("section")
    slot_total = experts * capacity
    partial_logits = jnp.dot(tokens, w_router, preferred_element_type=jnp.float32)
    logits = lax.psum(partial_logits, "section")
    route_hot = routes[:, :, None] == jnp.arange(experts, dtype=jnp.int32)[None, None, :]
    zero_f = jnp.zeros((), jnp.float32)
    chosen = jnp.sum(jnp.where(route_hot, logits[:, None, :], zero_f), axis=2)
    gate_first = 1.0 / (1.0 + jnp.exp(chosen[:, 1] - chosen[:, 0]))
    gate_second = 1.0 / (1.0 + jnp.exp(chosen[:, 0] - chosen[:, 1]))
    counts_flat = route_hot.astype(jnp.int32).reshape(2 * tok_count, experts)
    earlier = jnp.cumsum(counts_flat, axis=0) - counts_flat
    position = jnp.sum(earlier * counts_flat, axis=1).reshape(tok_count, 2)
    slot_row = routes * capacity + position
    slot_ids = jnp.arange(slot_total, dtype=jnp.int32)[None, :]
    pick_first = slot_row[:, 0:1] == slot_ids
    pick_second = slot_row[:, 1:2] == slot_ids
    pick_both = (pick_first | pick_second).astype(jnp.bfloat16)
    x_source = jnp.einsum(
        "ts,td->sd", pick_both, tokens, preferred_element_type=jnp.float32
    ).astype(jnp.bfloat16)
    cot_float = cotangent.astype(jnp.float32)
    scaled_first = (gate_first[:, None] * cot_float).astype(jnp.bfloat16)
    scaled_second = (gate_second[:, None] * cot_float).astype(jnp.bfloat16)
    dy_source = jnp.einsum(
        "ts,td->sd",
        pick_first.astype(jnp.bfloat16),
        scaled_first,
        preferred_element_type=jnp.float32,
    )
    dy_source = dy_source + jnp.einsum(
        "ts,td->sd",
        pick_second.astype(jnp.bfloat16),
        scaled_second,
        preferred_element_type=jnp.float32,
    )
    dy_source = dy_source.astype(jnp.bfloat16)
    both_source = jnp.stack(
        [x_source.reshape(experts, capacity * width), dy_source.reshape(experts, capacity * width)],
        axis=1,
    )
    block_rows = 2 * capacity * width // LANES
    sent = jnp.broadcast_to(
        both_source.reshape(experts, 1, block_rows, LANES), (experts, groups, block_rows, LANES)
    ).reshape(experts * groups, block_rows, LANES)
    received = lax.all_to_all(sent, EXPERT_AXES, 0, 0, tiled=True)
    row_total = received.shape[0] * capacity
    half = block_rows // 2
    x_recv = received[:, :half].reshape(row_total, width)
    dy_recv = received[:, half:].reshape(row_total, width)
    x_rows = lax.all_gather(x_recv, "section", axis=1, tiled=True)
    dy_rows = lax.all_gather(dy_recv, "section", axis=1, tiled=True)
    gate_local = w_gate[0]
    up_local = w_up[0]
    down_local = w_down[0]
    pre_gate = jnp.dot(x_rows, gate_local, preferred_element_type=jnp.float32)
    pre_up = jnp.dot(x_rows, up_local, preferred_element_type=jnp.float32)
    sigmoid_gate = jax.nn.sigmoid(pre_gate)
    activated = pre_gate * sigmoid_gate
    hidden = (activated * pre_up).astype(jnp.bfloat16)
    hid = gate_local.shape[1]
    down_blocks = down_local.reshape(hid, n_section, width)
    gate_blocks = gate_local.reshape(n_section, width, hid)
    up_blocks = up_local.reshape(n_section, width, hid)
    out_piece = jnp.einsum("pf,fsd->spd", hidden, down_blocks, preferred_element_type=jnp.float32)
    out_piece = out_piece.astype(jnp.bfloat16).reshape(n_section * row_total, width)
    out_piece, dy_rows = lax.optimization_barrier((out_piece, dy_rows))
    out_red = lax.psum_scatter(out_piece, "section", scatter_dimension=0, tiled=True)
    n_dev = row_total // capacity
    out_back = lax.all_to_all(out_red.reshape(n_dev, half, LANES), EXPERT_AXES, 0, 0, tiled=True)
    out_back = out_back.reshape(experts, groups, capacity, width).astype(jnp.float32)
    slot_out = jnp.sum(out_back, axis=1).reshape(slot_total, width)
    d_hidden = jnp.einsum("pd,fd->pf", dy_rows, down_local, preferred_element_type=jnp.float32)
    grad_down = jnp.einsum("pf,pd->fd", hidden, dy_rows, preferred_element_type=jnp.float32).astype(
        jnp.bfloat16
    )
    d_pre_gate = (
        d_hidden * pre_up * sigmoid_gate * (1.0 + pre_gate * (1.0 - sigmoid_gate))
    ).astype(jnp.bfloat16)
    d_pre_up = (d_hidden * activated).astype(jnp.bfloat16)
    grad_gate = jnp.einsum(
        "pd,pf->df", x_rows, d_pre_gate, preferred_element_type=jnp.float32
    ).astype(jnp.bfloat16)
    grad_up = jnp.einsum("pd,pf->df", x_rows, d_pre_up, preferred_element_type=jnp.float32).astype(
        jnp.bfloat16
    )
    first_float = pick_first.astype(jnp.float32)
    second_float = pick_second.astype(jnp.float32)
    out_first = jnp.dot(first_float, slot_out, precision=highest)
    out_second = jnp.dot(second_float, slot_out, precision=highest)
    mixed = (gate_first[:, None] * out_first + gate_second[:, None] * out_second).astype(
        jnp.bfloat16
    )
    local_inner = jnp.stack(
        [jnp.sum(cot_float * out_first, axis=1), jnp.sum(cot_float * out_second, axis=1)], axis=1
    )
    gate_inner = lax.psum(local_inner, "section")
    d_first = gate_first * gate_second * (gate_inner[:, 0] - gate_inner[:, 1])
    d_logits = jnp.where(route_hot[:, 0, :], d_first[:, None], zero_f) - jnp.where(
        route_hot[:, 1, :], d_first[:, None], zero_f
    )
    dx_piece = jnp.einsum("pf,sdf->spd", d_pre_gate, gate_blocks, preferred_element_type=jnp.float32)
    dx_piece = dx_piece + jnp.einsum(
        "pf,sdf->spd", d_pre_up, up_blocks, preferred_element_type=jnp.float32
    )
    dx_red = lax.psum_scatter(
        dx_piece.astype(jnp.bfloat16).reshape(n_section * row_total, width),
        "section",
        scatter_dimension=0,
        tiled=True,
    )
    dx_back = lax.all_to_all(dx_red.reshape(n_dev, half, LANES), EXPERT_AXES, 0, 0, tiled=True)
    dx_back = dx_back.reshape(experts, groups, capacity, width).astype(jnp.float32)
    slot_dx = jnp.sum(dx_back, axis=1).reshape(slot_total, width)
    dx_expert = jnp.dot(first_float, slot_dx, precision=highest)
    dx_expert = dx_expert + jnp.dot(second_float, slot_dx, precision=highest)
    router_float = w_router.astype(jnp.float32)
    grad_tokens = (dx_expert + jnp.dot(d_logits, router_float.T, precision=highest)).astype(
        jnp.bfloat16
    )
    router_part = jnp.einsum(
        "te,tf->ef", d_logits, tokens.astype(jnp.float32), precision=highest
    )
    router_part = lax.psum(router_part, EXPERT_AXES[2])
    for name in (EXPERT_AXES[1], EXPERT_AXES[0]):
        router_part = jnp.sum(lax.all_gather(router_part, name, axis=0), axis=0)
    grad_router = router_part.T
    return (mixed, grad_tokens, grad_router, grad_gate[None], grad_up[None], grad_down[None])


def expert_shape(devices):
    try:
        xs = sorted({d.coords[0] for d in devices.flat})
        zs = sorted({d.coords[2] for d in devices.flat})
        cores = sorted({d.core_on_chip for d in devices.flat})
        shape = (len(xs), len(zs), len(cores))
    except AttributeError:
        shape = (4, 8, 2)
    if int(np.prod(shape)) != devices.shape[1]:
        shape = (devices.shape[1] // 16, 8, 2)
    return shape


def solution(mesh):
    devices = mesh.devices
    fine = Mesh(
        devices.reshape((devices.shape[0],) + expert_shape(devices)),
        ("section",) + EXPERT_AXES,
    )
    ex = EXPERT_AXES
    in_specs = (
        P(ex, "section"),
        P(ex, "section"),
        P(ex, None),
        P("section", None),
        P(ex, None, "section"),
        P(ex, None, "section"),
        P(ex, "section", None),
    )
    out_specs = (
        P(ex, "section"),
        P(ex, "section"),
        P("section", None),
        P(ex, None, "section"),
        P(ex, None, "section"),
        P(ex, "section", None),
    )
    return jax.shard_map(
        per_device, mesh=fine, in_specs=in_specs, out_specs=out_specs, check_vma=False
    )
```

```python
import jax
import jax.numpy as jnp
import numpy as np
from jax import lax
from jax.sharding import Mesh
from jax.sharding import PartitionSpec as P

CAP = 6
LANES = 128
EXPERT_AXES = ("ex", "ez", "ec")


def expert_size():
    size = 1
    for name in EXPERT_AXES:
        size = size * lax.axis_size(name)
    return size


def per_device(tokens, cotangent, routes, w_router, w_gate, w_up, w_down):
    highest = lax.Precision.HIGHEST
    experts = w_router.shape[1]
    groups = expert_size() // experts
    capacity = CAP
    tok_count, width = tokens.shape
    n_section = lax.axis_size("section")
    slot_total = experts * capacity
    partial_logits = jnp.dot(tokens, w_router, preferred_element_type=jnp.float32)
    logits = lax.psum(partial_logits, "section")
    route_hot = routes[:, :, None] == jnp.arange(experts, dtype=jnp.int32)[None, None, :]
    zero_f = jnp.zeros((), jnp.float32)
    chosen = jnp.sum(jnp.where(route_hot, logits[:, None, :], zero_f), axis=2)
    gate_first = 1.0 / (1.0 + jnp.exp(chosen[:, 1] - chosen[:, 0]))
    gate_second = 1.0 / (1.0 + jnp.exp(chosen[:, 0] - chosen[:, 1]))
    counts_flat = route_hot.astype(jnp.int32).reshape(2 * tok_count, experts)
    earlier = jnp.cumsum(counts_flat, axis=0) - counts_flat
    position = jnp.sum(earlier * counts_flat, axis=1).reshape(tok_count, 2)
    slot_row = routes * capacity + position
    slot_ids = jnp.arange(slot_total, dtype=jnp.int32)[None, :]
    pick_first = slot_row[:, 0:1] == slot_ids
    pick_second = slot_row[:, 1:2] == slot_ids
    pick_both = (pick_first | pick_second).astype(jnp.bfloat16)
    x_source = jnp.einsum(
        "ts,td->sd", pick_both, tokens, preferred_element_type=jnp.float32
    ).astype(jnp.bfloat16)
    cot_float = cotangent.astype(jnp.float32)
    scaled_first = (gate_first[:, None] * cot_float).astype(jnp.bfloat16)
    scaled_second = (gate_second[:, None] * cot_float).astype(jnp.bfloat16)
    dy_source = jnp.einsum(
        "ts,td->sd",
        pick_first.astype(jnp.bfloat16),
        scaled_first,
        preferred_element_type=jnp.float32,
    )
    dy_source = dy_source + jnp.einsum(
        "ts,td->sd",
        pick_second.astype(jnp.bfloat16),
        scaled_second,
        preferred_element_type=jnp.float32,
    )
    dy_source = dy_source.astype(jnp.bfloat16)
    both_source = jnp.stack(
        [x_source.reshape(experts, capacity * width), dy_source.reshape(experts, capacity * width)],
        axis=1,
    )
    block_rows = 2 * capacity * width // LANES
    sent = jnp.broadcast_to(
        both_source.reshape(experts, 1, block_rows, LANES), (experts, groups, block_rows, LANES)
    ).reshape(experts * groups, block_rows, LANES)
    received = lax.all_to_all(sent, EXPERT_AXES, 0, 0, tiled=True)
    row_total = received.shape[0] * capacity
    half = block_rows // 2
    x_recv = received[:, :half].reshape(row_total, width)
    dy_recv = received[:, half:].reshape(row_total, width)
    x_rows = lax.all_gather(x_recv, "section", axis=1, tiled=True)
    dy_rows = lax.all_gather(dy_recv, "section", axis=1, tiled=True)
    gate_local = w_gate[0]
    up_local = w_up[0]
    down_local = w_down[0]
    pre_gate = jnp.dot(x_rows, gate_local, preferred_element_type=jnp.float32)
    pre_up = jnp.dot(x_rows, up_local, preferred_element_type=jnp.float32)
    sigmoid_gate = jax.nn.sigmoid(pre_gate)
    activated = pre_gate * sigmoid_gate
    hidden = (activated * pre_up).astype(jnp.bfloat16)
    hid = gate_local.shape[1]
    down_blocks = down_local.reshape(hid, n_section, width)
    gate_blocks = gate_local.reshape(n_section, width, hid)
    up_blocks = up_local.reshape(n_section, width, hid)
    out_piece = jnp.einsum("pf,fsd->spd", hidden, down_blocks, preferred_element_type=jnp.float32)
    out_piece = out_piece.astype(jnp.bfloat16).reshape(n_section * row_total, width)
    out_piece, dy_rows = lax.optimization_barrier((out_piece, dy_rows))
    out_red = lax.psum_scatter(out_piece, "section", scatter_dimension=0, tiled=True)
    n_dev = row_total // capacity
    out_back = lax.all_to_all(out_red.reshape(n_dev, half, LANES), EXPERT_AXES, 0, 0, tiled=True)
    out_back = out_back.reshape(experts, groups, capacity, width).astype(jnp.float32)
    slot_out = jnp.sum(out_back, axis=1).reshape(slot_total, width)
    d_hidden = jnp.einsum("pd,fd->pf", dy_rows, down_local, preferred_element_type=jnp.float32)
    grad_down = jnp.einsum("pf,pd->fd", hidden, dy_rows, preferred_element_type=jnp.float32).astype(
        jnp.bfloat16
    )
    d_pre_gate = (
        d_hidden * pre_up * sigmoid_gate * (1.0 + pre_gate * (1.0 - sigmoid_gate))
    ).astype(jnp.bfloat16)
    d_pre_up = (d_hidden * activated).astype(jnp.bfloat16)
    grad_gate = jnp.einsum(
        "pd,pf->df", x_rows, d_pre_gate, preferred_element_type=jnp.float32
    ).astype(jnp.bfloat16)
    grad_up = jnp.einsum("pd,pf->df", x_rows, d_pre_up, preferred_element_type=jnp.float32).astype(
        jnp.bfloat16
    )
    first_float = pick_first.astype(jnp.float32)
    second_float = pick_second.astype(jnp.float32)
    out_first = jnp.dot(first_float, slot_out, precision=highest)
    out_second = jnp.dot(second_float, slot_out, precision=highest)
    mixed = (gate_first[:, None] * out_first + gate_second[:, None] * out_second).astype(
        jnp.bfloat16
    )
    local_inner = jnp.stack(
        [jnp.sum(cot_float * out_first, axis=1), jnp.sum(cot_float * out_second, axis=1)], axis=1
    )
    dx_piece = jnp.einsum("pf,sdf->spd", d_pre_gate, gate_blocks, preferred_element_type=jnp.float32)
    dx_piece = dx_piece + jnp.einsum(
        "pf,sdf->spd", d_pre_up, up_blocks, preferred_element_type=jnp.float32
    )
    dx_red = lax.psum_scatter(
        dx_piece.astype(jnp.bfloat16).reshape(n_section * row_total, width),
        "section",
        scatter_dimension=0,
        tiled=True,
    )
    gate_inner = lax.psum(local_inner, "section")
    gate_inner, dx_red = lax.optimization_barrier((gate_inner, dx_red))
    dx_back = lax.all_to_all(dx_red.reshape(n_dev, half, LANES), EXPERT_AXES, 0, 0, tiled=True)
    d_first = gate_first * gate_second * (gate_inner[:, 0] - gate_inner[:, 1])
    d_logits = jnp.where(route_hot[:, 0, :], d_first[:, None], zero_f) - jnp.where(
        route_hot[:, 1, :], d_first[:, None], zero_f
    )
    dx_back = dx_back.reshape(experts, groups, capacity, width).astype(jnp.float32)
    slot_dx = jnp.sum(dx_back, axis=1).reshape(slot_total, width)
    dx_expert = jnp.dot(first_float, slot_dx, precision=highest)
    dx_expert = dx_expert + jnp.dot(second_float, slot_dx, precision=highest)
    router_float = w_router.astype(jnp.float32)
    grad_tokens = (dx_expert + jnp.dot(d_logits, router_float.T, precision=highest)).astype(
        jnp.bfloat16
    )
    router_part = jnp.einsum(
        "te,tf->ef", d_logits, tokens.astype(jnp.float32), precision=highest
    )
    router_part = lax.psum(router_part, EXPERT_AXES[2])
    for name in (EXPERT_AXES[1], EXPERT_AXES[0]):
        router_part = jnp.sum(lax.all_gather(router_part, name, axis=0), axis=0)
    grad_router = router_part.T
    return (mixed, grad_tokens, grad_router, grad_gate[None], grad_up[None], grad_down[None])


def expert_shape(devices):
    try:
        xs = sorted({d.coords[0] for d in devices.flat})
        zs = sorted({d.coords[2] for d in devices.flat})
        cores = sorted({d.core_on_chip for d in devices.flat})
        shape = (len(xs), len(zs), len(cores))
    except AttributeError:
        shape = (4, 8, 2)
    if int(np.prod(shape)) != devices.shape[1]:
        shape = (devices.shape[1] // 16, 8, 2)
    return shape


def solution(mesh):
    devices = mesh.devices
    fine = Mesh(
        devices.reshape((devices.shape[0],) + expert_shape(devices)),
        ("section",) + EXPERT_AXES,
    )
    ex = EXPERT_AXES
    in_specs = (
        P(ex, "section"),
        P(ex, "section"),
        P(ex, None),
        P("section", None),
        P(ex, None, "section"),
        P(ex, None, "section"),
        P(ex, "section", None),
    )
    out_specs = (
        P(ex, "section"),
        P(ex, "section"),
        P("section", None),
        P(ex, None, "section"),
        P(ex, None, "section"),
        P(ex, "section", None),
    )
    return jax.shard_map(
        per_device, mesh=fine, in_specs=in_specs, out_specs=out_specs, check_vma=False
    )
```

```python
import jax
import jax.numpy as jnp
import numpy as np
from jax import lax
from jax.sharding import Mesh
from jax.sharding import PartitionSpec as P

CAP = 6
LANES = 128
EXPERT_AXES = ("ex", "ez", "ec")


def expert_size():
    size = 1
    for name in EXPERT_AXES:
        size = size * lax.axis_size(name)
    return size


def per_device(tokens, cotangent, routes, w_router, w_gate, w_up, w_down):
    highest = lax.Precision.HIGHEST
    experts = w_router.shape[1]
    groups = expert_size() // experts
    capacity = CAP
    tok_count, width = tokens.shape
    n_section = lax.axis_size("section")
    slot_total = experts * capacity
    partial_logits = jnp.dot(tokens, w_router, preferred_element_type=jnp.float32)
    logits = lax.psum(partial_logits, "section")
    route_hot = routes[:, :, None] == jnp.arange(experts, dtype=jnp.int32)[None, None, :]
    zero_f = jnp.zeros((), jnp.float32)
    chosen = jnp.sum(jnp.where(route_hot, logits[:, None, :], zero_f), axis=2)
    gate_first = 1.0 / (1.0 + jnp.exp(chosen[:, 1] - chosen[:, 0]))
    gate_second = 1.0 / (1.0 + jnp.exp(chosen[:, 0] - chosen[:, 1]))
    counts_flat = route_hot.astype(jnp.int32).reshape(2 * tok_count, experts)
    earlier = jnp.cumsum(counts_flat, axis=0) - counts_flat
    position = jnp.sum(earlier * counts_flat, axis=1).reshape(tok_count, 2)
    slot_row = routes * capacity + position
    slot_ids = jnp.arange(slot_total, dtype=jnp.int32)[None, :]
    pick_first = slot_row[:, 0:1] == slot_ids
    pick_second = slot_row[:, 1:2] == slot_ids
    pick_both = (pick_first | pick_second).astype(jnp.bfloat16)
    x_source = jnp.einsum(
        "ts,td->sd", pick_both, tokens, preferred_element_type=jnp.float32
    ).astype(jnp.bfloat16)
    cot_float = cotangent.astype(jnp.float32)
    scaled_first = (gate_first[:, None] * cot_float).astype(jnp.bfloat16)
    scaled_second = (gate_second[:, None] * cot_float).astype(jnp.bfloat16)
    dy_source = jnp.einsum(
        "ts,td->sd",
        pick_first.astype(jnp.bfloat16),
        scaled_first,
        preferred_element_type=jnp.float32,
    )
    dy_source = dy_source + jnp.einsum(
        "ts,td->sd",
        pick_second.astype(jnp.bfloat16),
        scaled_second,
        preferred_element_type=jnp.float32,
    )
    dy_source = dy_source.astype(jnp.bfloat16)
    both_source = jnp.stack(
        [x_source.reshape(experts, capacity * width), dy_source.reshape(experts, capacity * width)],
        axis=1,
    )
    block_rows = 2 * capacity * width // LANES
    sent = jnp.broadcast_to(
        both_source.reshape(experts, 1, block_rows, LANES), (experts, groups, block_rows, LANES)
    ).reshape(experts * groups, block_rows, LANES)
    received = lax.all_to_all(sent, EXPERT_AXES, 0, 0, tiled=True)
    row_total = received.shape[0] * capacity
    half = block_rows // 2
    x_recv = received[:, :half].reshape(row_total, width)
    dy_recv = received[:, half:].reshape(row_total, width)
    x_rows = lax.all_gather(x_recv, "section", axis=1, tiled=True)
    gate_local = w_gate[0]
    up_local = w_up[0]
    down_local = w_down[0]
    pre_gate = jnp.dot(x_rows, gate_local, preferred_element_type=jnp.float32)
    pre_up = jnp.dot(x_rows, up_local, preferred_element_type=jnp.float32)
    sigmoid_gate = jax.nn.sigmoid(pre_gate)
    activated = pre_gate * sigmoid_gate
    hidden = (activated * pre_up).astype(jnp.bfloat16)
    hid = gate_local.shape[1]
    down_blocks = down_local.reshape(hid, n_section, width)
    gate_blocks = gate_local.reshape(n_section, width, hid)
    up_blocks = up_local.reshape(n_section, width, hid)
    out_piece = jnp.einsum("pf,fsd->spd", hidden, down_blocks, preferred_element_type=jnp.float32)
    out_piece = out_piece.astype(jnp.bfloat16).reshape(n_section * row_total, width)
    out_red = lax.psum_scatter(out_piece, "section", scatter_dimension=0, tiled=True)
    out_red, dy_recv = lax.optimization_barrier((out_red, dy_recv))
    dy_rows = lax.all_gather(dy_recv, "section", axis=1, tiled=True)
    n_dev = row_total // capacity
    out_back = lax.all_to_all(out_red.reshape(n_dev, half, LANES), EXPERT_AXES, 0, 0, tiled=True)
    out_back = out_back.reshape(experts, groups, capacity, width).astype(jnp.float32)
    slot_out = jnp.sum(out_back, axis=1).reshape(slot_total, width)
    d_hidden = jnp.einsum("pd,fd->pf", dy_rows, down_local, preferred_element_type=jnp.float32)
    grad_down = jnp.einsum("pf,pd->fd", hidden, dy_rows, preferred_element_type=jnp.float32).astype(
        jnp.bfloat16
    )
    d_pre_gate = (
        d_hidden * pre_up * sigmoid_gate * (1.0 + pre_gate * (1.0 - sigmoid_gate))
    ).astype(jnp.bfloat16)
    d_pre_up = (d_hidden * activated).astype(jnp.bfloat16)
    grad_gate = jnp.einsum(
        "pd,pf->df", x_rows, d_pre_gate, preferred_element_type=jnp.float32
    ).astype(jnp.bfloat16)
    grad_up = jnp.einsum("pd,pf->df", x_rows, d_pre_up, preferred_element_type=jnp.float32).astype(
        jnp.bfloat16
    )
    first_float = pick_first.astype(jnp.float32)
    second_float = pick_second.astype(jnp.float32)
    out_first = jnp.dot(first_float, slot_out, precision=highest)
    out_second = jnp.dot(second_float, slot_out, precision=highest)
    mixed = (gate_first[:, None] * out_first + gate_second[:, None] * out_second).astype(
        jnp.bfloat16
    )
    local_inner = jnp.stack(
        [jnp.sum(cot_float * out_first, axis=1), jnp.sum(cot_float * out_second, axis=1)], axis=1
    )
    dx_piece = jnp.einsum("pf,sdf->spd", d_pre_gate, gate_blocks, preferred_element_type=jnp.float32)
    dx_piece = dx_piece + jnp.einsum(
        "pf,sdf->spd", d_pre_up, up_blocks, preferred_element_type=jnp.float32
    )
    gate_inner = lax.psum(local_inner, "section")
    d_first = gate_first * gate_second * (gate_inner[:, 0] - gate_inner[:, 1])
    d_logits = jnp.where(route_hot[:, 0, :], d_first[:, None], zero_f) - jnp.where(
        route_hot[:, 1, :], d_first[:, None], zero_f
    )
    dx_piece = dx_piece.astype(jnp.bfloat16).reshape(n_section * row_total, width)
    d_logits, dx_piece = lax.optimization_barrier((d_logits, dx_piece))
    dx_red = lax.psum_scatter(dx_piece, "section", scatter_dimension=0, tiled=True)
    router_part = jnp.einsum(
        "te,tf->ef", d_logits, tokens.astype(jnp.float32), precision=highest
    )
    router_part = lax.psum(router_part, EXPERT_AXES[2])
    for name in (EXPERT_AXES[1], EXPERT_AXES[0]):
        router_part = jnp.sum(lax.all_gather(router_part, name, axis=0), axis=0)
    router_part, dx_red = lax.optimization_barrier((router_part, dx_red))
    dx_back = lax.all_to_all(dx_red.reshape(n_dev, half, LANES), EXPERT_AXES, 0, 0, tiled=True)
    dx_back = dx_back.reshape(experts, groups, capacity, width).astype(jnp.float32)
    slot_dx = jnp.sum(dx_back, axis=1).reshape(slot_total, width)
    dx_expert = jnp.dot(first_float, slot_dx, precision=highest)
    dx_expert = dx_expert + jnp.dot(second_float, slot_dx, precision=highest)
    router_float = w_router.astype(jnp.float32)
    grad_tokens = (dx_expert + jnp.dot(d_logits, router_float.T, precision=highest)).astype(
        jnp.bfloat16
    )
    grad_router = router_part.T
    return (mixed, grad_tokens, grad_router, grad_gate[None], grad_up[None], grad_down[None])


def expert_shape(devices):
    try:
        xs = sorted({d.coords[0] for d in devices.flat})
        zs = sorted({d.coords[2] for d in devices.flat})
        cores = sorted({d.core_on_chip for d in devices.flat})
        shape = (len(xs), len(zs), len(cores))
    except AttributeError:
        shape = (4, 8, 2)
    if int(np.prod(shape)) != devices.shape[1]:
        shape = (devices.shape[1] // 16, 8, 2)
    return shape


def solution(mesh):
    devices = mesh.devices
    fine = Mesh(
        devices.reshape((devices.shape[0],) + expert_shape(devices)),
        ("section",) + EXPERT_AXES,
    )
    ex = EXPERT_AXES
    in_specs = (
        P(ex, "section"),
        P(ex, "section"),
        P(ex, None),
        P("section", None),
        P(ex, None, "section"),
        P(ex, None, "section"),
        P(ex, "section", None),
    )
    out_specs = (
        P(ex, "section"),
        P(ex, "section"),
        P("section", None),
        P(ex, None, "section"),
        P(ex, None, "section"),
        P(ex, "section", None),
    )
    return jax.shard_map(
        per_device, mesh=fine, in_specs=in_specs, out_specs=out_specs, check_vma=False
    )
```

```python
import jax
import jax.numpy as jnp
import numpy as np
from jax import lax
from jax.sharding import Mesh
from jax.sharding import PartitionSpec as P

CAP = 6
LANES = 128
EXPERT_AXES = ("ex", "ez", "ec")


def expert_size():
    size = 1
    for name in EXPERT_AXES:
        size = size * lax.axis_size(name)
    return size


def per_device(tokens, cotangent, routes, w_router, w_gate, w_up, w_down):
    highest = lax.Precision.HIGHEST
    experts = w_router.shape[1]
    groups = expert_size() // experts
    capacity = CAP
    tok_count, width = tokens.shape
    n_section = lax.axis_size("section")
    slot_total = experts * capacity
    partial_logits = jnp.dot(tokens, w_router, preferred_element_type=jnp.float32)
    logits = lax.psum(partial_logits, "section")
    route_hot = routes[:, :, None] == jnp.arange(experts, dtype=jnp.int32)[None, None, :]
    zero_f = jnp.zeros((), jnp.float32)
    chosen = jnp.sum(jnp.where(route_hot, logits[:, None, :], zero_f), axis=2)
    gate_first = 1.0 / (1.0 + jnp.exp(chosen[:, 1] - chosen[:, 0]))
    gate_second = 1.0 / (1.0 + jnp.exp(chosen[:, 0] - chosen[:, 1]))
    counts_flat = route_hot.astype(jnp.int32).reshape(2 * tok_count, experts)
    earlier = jnp.cumsum(counts_flat, axis=0) - counts_flat
    position = jnp.sum(earlier * counts_flat, axis=1).reshape(tok_count, 2)
    slot_row = routes * capacity + position
    slot_ids = jnp.arange(slot_total, dtype=jnp.int32)[None, :]
    pick_first = slot_row[:, 0:1] == slot_ids
    pick_second = slot_row[:, 1:2] == slot_ids
    pick_both = (pick_first | pick_second).astype(jnp.bfloat16)
    both_rows = jnp.concatenate([tokens, cotangent], axis=1)
    selected = jnp.einsum(
        "ts,td->sd", pick_both, both_rows, preferred_element_type=jnp.float32
    ).astype(jnp.bfloat16)
    x_source = selected[:, :width]
    cot_source = selected[:, width:].astype(jnp.float32)
    cot_float = cotangent.astype(jnp.float32)
    zero_gate = jnp.zeros((), jnp.float32)
    gate_slot = jnp.sum(
        jnp.where(pick_first, gate_first[:, None], zero_gate)
        + jnp.where(pick_second, gate_second[:, None], zero_gate),
        axis=0,
    )
    dy_source = (gate_slot[:, None] * cot_source).astype(jnp.bfloat16)
    both_source = jnp.stack(
        [x_source.reshape(experts, capacity * width), dy_source.reshape(experts, capacity * width)],
        axis=1,
    )
    block_rows = 2 * capacity * width // LANES
    sent = jnp.broadcast_to(
        both_source.reshape(experts, 1, block_rows, LANES), (experts, groups, block_rows, LANES)
    ).reshape(experts * groups, block_rows, LANES)
    received = lax.all_to_all(sent, EXPERT_AXES, 0, 0, tiled=True)
    row_total = received.shape[0] * capacity
    half = block_rows // 2
    x_recv = received[:, :half].reshape(row_total, width)
    dy_recv = received[:, half:].reshape(row_total, width)
    x_rows = lax.all_gather(x_recv, "section", axis=1, tiled=True)
    gate_local = w_gate[0]
    up_local = w_up[0]
    down_local = w_down[0]
    pre_gate = jnp.dot(x_rows, gate_local, preferred_element_type=jnp.float32)
    pre_up = jnp.dot(x_rows, up_local, preferred_element_type=jnp.float32)
    sigmoid_gate = jax.nn.sigmoid(pre_gate)
    activated = pre_gate * sigmoid_gate
    hidden = (activated * pre_up).astype(jnp.bfloat16)
    hid = gate_local.shape[1]
    down_blocks = down_local.reshape(hid, n_section, width)
    gate_blocks = gate_local.reshape(n_section, width, hid)
    up_blocks = up_local.reshape(n_section, width, hid)
    out_piece = jnp.einsum("pf,fsd->spd", hidden, down_blocks, preferred_element_type=jnp.float32)
    out_piece = out_piece.astype(jnp.bfloat16).reshape(n_section * row_total, width)
    out_red = lax.psum_scatter(out_piece, "section", scatter_dimension=0, tiled=True)
    out_red, dy_recv = lax.optimization_barrier((out_red, dy_recv))
    dy_rows = lax.all_gather(dy_recv, "section", axis=1, tiled=True)
    n_dev = row_total // capacity
    out_back = lax.all_to_all(out_red.reshape(n_dev, half, LANES), EXPERT_AXES, 0, 0, tiled=True)
    out_back = out_back.reshape(experts, groups, half, LANES).astype(jnp.float32)
    slot_out = jnp.sum(out_back, axis=1).reshape(slot_total, width)
    d_hidden = jnp.einsum("pd,fd->pf", dy_rows, down_local, preferred_element_type=jnp.float32)
    grad_down = jnp.einsum("pf,pd->fd", hidden, dy_rows, preferred_element_type=jnp.float32).astype(
        jnp.bfloat16
    )
    d_pre_gate = (
        d_hidden * pre_up * sigmoid_gate * (1.0 + pre_gate * (1.0 - sigmoid_gate))
    ).astype(jnp.bfloat16)
    d_pre_up = (d_hidden * activated).astype(jnp.bfloat16)
    grad_gate = jnp.einsum(
        "pd,pf->df", x_rows, d_pre_gate, preferred_element_type=jnp.float32
    ).astype(jnp.bfloat16)
    grad_up = jnp.einsum("pd,pf->df", x_rows, d_pre_up, preferred_element_type=jnp.float32).astype(
        jnp.bfloat16
    )
    first_float = pick_first.astype(jnp.float32)
    second_float = pick_second.astype(jnp.float32)
    out_first = jnp.dot(first_float, slot_out, precision=highest)
    out_second = jnp.dot(second_float, slot_out, precision=highest)
    mixed = (gate_first[:, None] * out_first + gate_second[:, None] * out_second).astype(
        jnp.bfloat16
    )
    local_inner = jnp.stack(
        [jnp.sum(cot_float * out_first, axis=1), jnp.sum(cot_float * out_second, axis=1)], axis=1
    )
    dx_piece = jnp.einsum("pf,sdf->spd", d_pre_gate, gate_blocks, preferred_element_type=jnp.float32)
    dx_piece = dx_piece + jnp.einsum(
        "pf,sdf->spd", d_pre_up, up_blocks, preferred_element_type=jnp.float32
    )
    gate_inner = lax.psum(local_inner, "section")
    d_first = gate_first * gate_second * (gate_inner[:, 0] - gate_inner[:, 1])
    d_logits = jnp.where(route_hot[:, 0, :], d_first[:, None], zero_f) - jnp.where(
        route_hot[:, 1, :], d_first[:, None], zero_f
    )
    dx_piece = dx_piece.astype(jnp.bfloat16).reshape(n_section * row_total, width)
    d_logits, dx_piece = lax.optimization_barrier((d_logits, dx_piece))
    dx_red = lax.psum_scatter(dx_piece, "section", scatter_dimension=0, tiled=True)
    router_part = jnp.einsum(
        "te,tf->ef", d_logits, tokens.astype(jnp.float32), precision=highest
    )
    router_part = lax.psum(router_part, EXPERT_AXES[2])
    for name in (EXPERT_AXES[1], EXPERT_AXES[0]):
        router_part = jnp.sum(lax.all_gather(router_part, name, axis=0), axis=0)
    router_part, dx_red = lax.optimization_barrier((router_part, dx_red))
    dx_back = lax.all_to_all(dx_red.reshape(n_dev, half, LANES), EXPERT_AXES, 0, 0, tiled=True)
    dx_back = dx_back.reshape(experts, groups, half, LANES).astype(jnp.float32)
    slot_dx = jnp.sum(dx_back, axis=1).reshape(slot_total, width)
    dx_expert = jnp.dot(first_float, slot_dx, precision=highest)
    dx_expert = dx_expert + jnp.dot(second_float, slot_dx, precision=highest)
    router_float = w_router.astype(jnp.float32)
    grad_tokens = (dx_expert + jnp.dot(d_logits, router_float.T, precision=highest)).astype(
        jnp.bfloat16
    )
    grad_router = router_part.T
    return (mixed, grad_tokens, grad_router, grad_gate[None], grad_up[None], grad_down[None])


def expert_shape(devices):
    try:
        xs = sorted({d.coords[0] for d in devices.flat})
        zs = sorted({d.coords[2] for d in devices.flat})
        cores = sorted({d.core_on_chip for d in devices.flat})
        shape = (len(xs), len(zs), len(cores))
    except AttributeError:
        shape = (4, 8, 2)
    if int(np.prod(shape)) != devices.shape[1]:
        shape = (devices.shape[1] // 16, 8, 2)
    return shape


def solution(mesh):
    devices = mesh.devices
    fine = Mesh(
        devices.reshape((devices.shape[0],) + expert_shape(devices)),
        ("section",) + EXPERT_AXES,
    )
    ex = EXPERT_AXES
    in_specs = (
        P(ex, "section"),
        P(ex, "section"),
        P(ex, None),
        P("section", None),
        P(ex, None, "section"),
        P(ex, None, "section"),
        P(ex, "section", None),
    )
    out_specs = (
        P(ex, "section"),
        P(ex, "section"),
        P("section", None),
        P(ex, None, "section"),
        P(ex, None, "section"),
        P(ex, "section", None),
    )
    return jax.shard_map(
        per_device, mesh=fine, in_specs=in_specs, out_specs=out_specs, check_vma=False
    )
```

```python
import jax
import jax.numpy as jnp
import numpy as np
from jax import lax
from jax.sharding import Mesh
from jax.sharding import PartitionSpec as P

CAP = 6
LANES = 128
EXPERT_AXES = ("ex", "ez", "ec")


def expert_size():
    size = 1
    for name in EXPERT_AXES:
        size = size * lax.axis_size(name)
    return size


def per_device(tokens, cotangent, routes, w_router, w_gate, w_up, w_down):
    highest = lax.Precision.HIGHEST
    experts = w_router.shape[1]
    groups = expert_size() // experts
    capacity = CAP
    tok_count, width = tokens.shape
    n_section = lax.axis_size("section")
    slot_total = experts * capacity
    route_hot = routes[:, :, None] == jnp.arange(experts, dtype=jnp.int32)[None, None, :]
    zero_f = jnp.zeros((), jnp.float32)
    counts_flat = route_hot.astype(jnp.int32).reshape(2 * tok_count, experts)
    earlier = jnp.cumsum(counts_flat, axis=0) - counts_flat
    position = jnp.sum(earlier * counts_flat, axis=1).reshape(tok_count, 2)
    slot_row = routes * capacity + position
    slot_ids = jnp.arange(slot_total, dtype=jnp.int32)[None, :]
    pick_first = slot_row[:, 0:1] == slot_ids
    pick_second = slot_row[:, 1:2] == slot_ids
    pick_both = (pick_first | pick_second).astype(jnp.bfloat16)
    both_rows = jnp.concatenate([tokens, cotangent], axis=1)
    selected = jnp.einsum(
        "ts,td->sd", pick_both, both_rows, preferred_element_type=jnp.float32
    ).astype(jnp.bfloat16)
    zero_i = jnp.zeros((), jnp.int32)
    other_slot = jnp.sum(
        jnp.where(pick_first, routes[:, 1:2], zero_i) + jnp.where(pick_second, routes[:, 0:1], zero_i),
        axis=0,
    )
    half = capacity * width // LANES
    meta = jnp.zeros((experts, 16, LANES), jnp.bfloat16)
    meta = meta.at[:, 0, :capacity].set(other_slot.reshape(experts, capacity).astype(jnp.bfloat16))
    both_source = jnp.concatenate(
        [
            selected[:, :width].reshape(experts, half, LANES),
            selected[:, width:].reshape(experts, half, LANES),
            meta,
        ],
        axis=1,
    )
    block_rows = both_source.shape[1]
    sent = jnp.broadcast_to(
        both_source[:, None], (experts, groups, block_rows, LANES)
    ).reshape(experts * groups, block_rows, LANES)
    received = lax.all_to_all(sent, EXPERT_AXES, 0, 0, tiled=True)
    row_total = received.shape[0] * capacity
    x_recv = received[:, :half].reshape(row_total, width)
    x_rows = lax.all_gather(x_recv, "section", axis=1, tiled=True)
    cot_recv = received[:, half : 2 * half].reshape(row_total, width)
    other_recv = received[:, 2 * half, :capacity].astype(jnp.int32).reshape(row_total)
    w_router, x_recv = lax.optimization_barrier((w_router, x_recv))
    partial_logits = jnp.dot(tokens, w_router, preferred_element_type=jnp.float32)
    logits = lax.psum(partial_logits, "section")
    chosen = jnp.sum(jnp.where(route_hot, logits[:, None, :], zero_f), axis=2)
    gate_first = 1.0 / (1.0 + jnp.exp(chosen[:, 1] - chosen[:, 0]))
    gate_second = 1.0 / (1.0 + jnp.exp(chosen[:, 0] - chosen[:, 1]))
    cot_float = cotangent.astype(jnp.float32)
    row_logits = lax.psum(
        jnp.dot(x_recv, w_router, preferred_element_type=jnp.float32), "section"
    )
    own = lax.axis_index(EXPERT_AXES) // groups
    expert_ids = jnp.arange(experts, dtype=jnp.int32)[None, :]
    own_logit = jnp.sum(jnp.where(expert_ids == own, row_logits, zero_f), axis=1)
    other_logit = jnp.sum(jnp.where(expert_ids == other_recv[:, None], row_logits, zero_f), axis=1)
    row_gate = 1.0 / (1.0 + jnp.exp(other_logit - own_logit))
    gate_local = w_gate[0]
    up_local = w_up[0]
    down_local = w_down[0]
    pre_gate = jnp.dot(x_rows, gate_local, preferred_element_type=jnp.float32)
    pre_up = jnp.dot(x_rows, up_local, preferred_element_type=jnp.float32)
    sigmoid_gate = jax.nn.sigmoid(pre_gate)
    activated = pre_gate * sigmoid_gate
    hidden = (activated * pre_up).astype(jnp.bfloat16)
    hid = gate_local.shape[1]
    down_blocks = down_local.reshape(hid, n_section, width)
    gate_blocks = gate_local.reshape(n_section, width, hid)
    up_blocks = up_local.reshape(n_section, width, hid)
    out_piece = jnp.einsum("pf,fsd->spd", hidden, down_blocks, preferred_element_type=jnp.float32)
    out_piece = out_piece.astype(jnp.bfloat16).reshape(n_section * row_total, width)
    out_red = lax.psum_scatter(out_piece, "section", scatter_dimension=0, tiled=True)
    out_red, cot_recv = lax.optimization_barrier((out_red, cot_recv))
    cot_rows = lax.all_gather(cot_recv, "section", axis=1, tiled=True)
    dy_rows = (row_gate[:, None] * cot_rows.astype(jnp.float32)).astype(jnp.bfloat16)
    n_dev = row_total // capacity
    out_back = lax.all_to_all(out_red.reshape(n_dev, half, LANES), EXPERT_AXES, 0, 0, tiled=True)
    out_back = out_back.reshape(experts, groups, half, LANES).astype(jnp.float32)
    slot_out = jnp.sum(out_back, axis=1).reshape(slot_total, width)
    d_hidden = jnp.einsum("pd,fd->pf", dy_rows, down_local, preferred_element_type=jnp.float32)
    grad_down = jnp.einsum("pf,pd->fd", hidden, dy_rows, preferred_element_type=jnp.float32).astype(
        jnp.bfloat16
    )
    d_pre_gate = (
        d_hidden * pre_up * sigmoid_gate * (1.0 + pre_gate * (1.0 - sigmoid_gate))
    ).astype(jnp.bfloat16)
    d_pre_up = (d_hidden * activated).astype(jnp.bfloat16)
    grad_gate = jnp.einsum(
        "pd,pf->df", x_rows, d_pre_gate, preferred_element_type=jnp.float32
    ).astype(jnp.bfloat16)
    grad_up = jnp.einsum("pd,pf->df", x_rows, d_pre_up, preferred_element_type=jnp.float32).astype(
        jnp.bfloat16
    )
    first_float = pick_first.astype(jnp.float32)
    second_float = pick_second.astype(jnp.float32)
    out_first = jnp.dot(first_float, slot_out, precision=highest)
    out_second = jnp.dot(second_float, slot_out, precision=highest)
    mixed = (gate_first[:, None] * out_first + gate_second[:, None] * out_second).astype(
        jnp.bfloat16
    )
    local_inner = jnp.stack(
        [jnp.sum(cot_float * out_first, axis=1), jnp.sum(cot_float * out_second, axis=1)], axis=1
    )
    dx_piece = jnp.einsum("pf,sdf->spd", d_pre_gate, gate_blocks, preferred_element_type=jnp.float32)
    dx_piece = dx_piece + jnp.einsum(
        "pf,sdf->spd", d_pre_up, up_blocks, preferred_element_type=jnp.float32
    )
    gate_inner = lax.psum(local_inner, "section")
    d_first = gate_first * gate_second * (gate_inner[:, 0] - gate_inner[:, 1])
    d_logits = jnp.where(route_hot[:, 0, :], d_first[:, None], zero_f) - jnp.where(
        route_hot[:, 1, :], d_first[:, None], zero_f
    )
    dx_piece = dx_piece.astype(jnp.bfloat16).reshape(n_section * row_total, width)
    d_logits, dx_piece = lax.optimization_barrier((d_logits, dx_piece))
    dx_red = lax.psum_scatter(dx_piece, "section", scatter_dimension=0, tiled=True)
    router_part = jnp.einsum(
        "te,tf->ef", d_logits, tokens.astype(jnp.float32), precision=highest
    )
    router_part = lax.psum(router_part, EXPERT_AXES[2])
    for name in (EXPERT_AXES[1], EXPERT_AXES[0]):
        router_part = jnp.sum(lax.all_gather(router_part, name, axis=0), axis=0)
    router_part, dx_red = lax.optimization_barrier((router_part, dx_red))
    dx_back = lax.all_to_all(dx_red.reshape(n_dev, half, LANES), EXPERT_AXES, 0, 0, tiled=True)
    dx_back = dx_back.reshape(experts, groups, half, LANES).astype(jnp.float32)
    slot_dx = jnp.sum(dx_back, axis=1).reshape(slot_total, width)
    dx_expert = jnp.dot(first_float, slot_dx, precision=highest)
    dx_expert = dx_expert + jnp.dot(second_float, slot_dx, precision=highest)
    router_float = w_router.astype(jnp.float32)
    grad_tokens = (dx_expert + jnp.dot(d_logits, router_float.T, precision=highest)).astype(
        jnp.bfloat16
    )
    grad_router = router_part.T
    return (mixed, grad_tokens, grad_router, grad_gate[None], grad_up[None], grad_down[None])


def expert_shape(devices):
    try:
        xs = sorted({d.coords[0] for d in devices.flat})
        zs = sorted({d.coords[2] for d in devices.flat})
        cores = sorted({d.core_on_chip for d in devices.flat})
        shape = (len(xs), len(zs), len(cores))
    except AttributeError:
        shape = (4, 8, 2)
    if int(np.prod(shape)) != devices.shape[1]:
        shape = (devices.shape[1] // 16, 8, 2)
    return shape


def solution(mesh):
    devices = mesh.devices
    fine = Mesh(
        devices.reshape((devices.shape[0],) + expert_shape(devices)),
        ("section",) + EXPERT_AXES,
    )
    ex = EXPERT_AXES
    in_specs = (
        P(ex, "section"),
        P(ex, "section"),
        P(ex, None),
        P("section", None),
        P(ex, None, "section"),
        P(ex, None, "section"),
        P(ex, "section", None),
    )
    out_specs = (
        P(ex, "section"),
        P(ex, "section"),
        P("section", None),
        P(ex, None, "section"),
        P(ex, None, "section"),
        P(ex, "section", None),
    )
    return jax.shard_map(
        per_device, mesh=fine, in_specs=in_specs, out_specs=out_specs, check_vma=False
    )
```

```python
import jax
import jax.numpy as jnp
import numpy as np
from jax import lax
from jax.sharding import Mesh
from jax.sharding import PartitionSpec as P

CAP = 6
LANES = 128
EXPERT_AXES = ("ex", "ez", "ec")


def expert_size():
    size = 1
    for name in EXPERT_AXES:
        size = size * lax.axis_size(name)
    return size


def per_device(tokens, cotangent, routes, w_router, w_gate, w_up, w_down):
    highest = lax.Precision.HIGHEST
    experts = w_router.shape[1]
    groups = expert_size() // experts
    capacity = CAP
    tok_count, width = tokens.shape
    n_section = lax.axis_size("section")
    slot_total = experts * capacity
    route_hot = routes[:, :, None] == jnp.arange(experts, dtype=jnp.int32)[None, None, :]
    zero_f = jnp.zeros((), jnp.float32)
    counts_flat = route_hot.astype(jnp.int32).reshape(2 * tok_count, experts)
    earlier = jnp.cumsum(counts_flat, axis=0) - counts_flat
    position = jnp.sum(earlier * counts_flat, axis=1).reshape(tok_count, 2)
    slot_row = routes * capacity + position
    slot_ids = jnp.arange(slot_total, dtype=jnp.int32)[None, :]
    pick_first = slot_row[:, 0:1] == slot_ids
    pick_second = slot_row[:, 1:2] == slot_ids
    pick_both = (pick_first | pick_second).astype(jnp.bfloat16)
    both_rows = jnp.concatenate([tokens, cotangent], axis=1)
    selected = jnp.einsum(
        "ts,td->sd", pick_both, both_rows, preferred_element_type=jnp.float32
    ).astype(jnp.bfloat16)
    zero_i = jnp.zeros((), jnp.int32)
    other_slot = jnp.sum(
        jnp.where(pick_first, routes[:, 1:2], zero_i) + jnp.where(pick_second, routes[:, 0:1], zero_i),
        axis=0,
    )
    half = capacity * width // LANES
    meta = jnp.zeros((experts, 16, LANES), jnp.bfloat16)
    meta = meta.at[:, 0, :capacity].set(other_slot.reshape(experts, capacity).astype(jnp.bfloat16))
    both_source = jnp.concatenate(
        [
            selected[:, :width].reshape(experts, half, LANES),
            selected[:, width:].reshape(experts, half, LANES),
            meta,
        ],
        axis=1,
    )
    block_rows = both_source.shape[1]
    sent = jnp.broadcast_to(
        both_source[:, None], (experts, groups, block_rows, LANES)
    ).reshape(experts * groups, block_rows, LANES)
    received = lax.all_to_all(sent, EXPERT_AXES, 0, 0, tiled=True)
    row_total = received.shape[0] * capacity
    x_recv = received[:, :half].reshape(row_total, width)
    x_rows = lax.all_gather(x_recv, "section", axis=1, tiled=True)
    cot_recv = received[:, half : 2 * half].reshape(row_total, width)
    other_recv = received[:, 2 * half, :capacity].astype(jnp.int32).reshape(row_total)
    w_router, x_recv = lax.optimization_barrier((w_router, x_recv))
    partial_logits = jnp.dot(tokens, w_router, preferred_element_type=jnp.float32)
    logits = lax.psum(partial_logits, "section")
    chosen = jnp.sum(jnp.where(route_hot, logits[:, None, :], zero_f), axis=2)
    gate_first = 1.0 / (1.0 + jnp.exp(chosen[:, 1] - chosen[:, 0]))
    gate_second = 1.0 / (1.0 + jnp.exp(chosen[:, 0] - chosen[:, 1]))
    cot_float = cotangent.astype(jnp.float32)
    row_logits = lax.psum(
        jnp.dot(x_recv, w_router, preferred_element_type=jnp.float32), "section"
    )
    own = lax.axis_index(EXPERT_AXES) // groups
    expert_ids = jnp.arange(experts, dtype=jnp.int32)[None, :]
    own_logit = jnp.sum(jnp.where(expert_ids == own, row_logits, zero_f), axis=1)
    other_logit = jnp.sum(jnp.where(expert_ids == other_recv[:, None], row_logits, zero_f), axis=1)
    row_gate = 1.0 / (1.0 + jnp.exp(other_logit - own_logit))
    row_gate, gate_first, gate_second, x_rows = lax.optimization_barrier(
        (row_gate, gate_first, gate_second, x_rows)
    )
    gate_local = w_gate[0]
    up_local = w_up[0]
    down_local = w_down[0]
    pre_gate = jnp.dot(x_rows, gate_local, preferred_element_type=jnp.float32)
    pre_up = jnp.dot(x_rows, up_local, preferred_element_type=jnp.float32)
    sigmoid_gate = jax.nn.sigmoid(pre_gate)
    activated = pre_gate * sigmoid_gate
    hidden = (activated * pre_up).astype(jnp.bfloat16)
    hid = gate_local.shape[1]
    down_blocks = down_local.reshape(hid, n_section, width)
    gate_blocks = gate_local.reshape(n_section, width, hid)
    up_blocks = up_local.reshape(n_section, width, hid)
    out_piece = jnp.einsum("pf,fsd->spd", hidden, down_blocks, preferred_element_type=jnp.float32)
    out_piece = out_piece.astype(jnp.bfloat16).reshape(n_section * row_total, width)
    out_red = lax.psum_scatter(out_piece, "section", scatter_dimension=0, tiled=True)
    out_red, cot_recv = lax.optimization_barrier((out_red, cot_recv))
    cot_rows = lax.all_gather(cot_recv, "section", axis=1, tiled=True)
    dy_rows = (row_gate[:, None] * cot_rows.astype(jnp.float32)).astype(jnp.bfloat16)
    n_dev = row_total // capacity
    out_back = lax.all_to_all(out_red.reshape(n_dev, half, LANES), EXPERT_AXES, 0, 0, tiled=True)
    out_back = out_back.reshape(experts, groups, half, LANES).astype(jnp.float32)
    slot_out = jnp.sum(out_back, axis=1).reshape(slot_total, width)
    d_hidden = jnp.einsum("pd,fd->pf", dy_rows, down_local, preferred_element_type=jnp.float32)
    grad_down = jnp.einsum("pf,pd->fd", hidden, dy_rows, preferred_element_type=jnp.float32).astype(
        jnp.bfloat16
    )
    d_pre_gate = (
        d_hidden * pre_up * sigmoid_gate * (1.0 + pre_gate * (1.0 - sigmoid_gate))
    ).astype(jnp.bfloat16)
    d_pre_up = (d_hidden * activated).astype(jnp.bfloat16)
    grad_gate = jnp.einsum(
        "pd,pf->df", x_rows, d_pre_gate, preferred_element_type=jnp.float32
    ).astype(jnp.bfloat16)
    grad_up = jnp.einsum("pd,pf->df", x_rows, d_pre_up, preferred_element_type=jnp.float32).astype(
        jnp.bfloat16
    )
    first_float = pick_first.astype(jnp.float32)
    second_float = pick_second.astype(jnp.float32)
    out_first = jnp.dot(first_float, slot_out, precision=highest)
    out_second = jnp.dot(second_float, slot_out, precision=highest)
    mixed = (gate_first[:, None] * out_first + gate_second[:, None] * out_second).astype(
        jnp.bfloat16
    )
    local_inner = jnp.stack(
        [jnp.sum(cot_float * out_first, axis=1), jnp.sum(cot_float * out_second, axis=1)], axis=1
    )
    dx_piece = jnp.einsum("pf,sdf->spd", d_pre_gate, gate_blocks, preferred_element_type=jnp.float32)
    dx_piece = dx_piece + jnp.einsum(
        "pf,sdf->spd", d_pre_up, up_blocks, preferred_element_type=jnp.float32
    )
    gate_inner = lax.psum(local_inner, "section")
    d_first = gate_first * gate_second * (gate_inner[:, 0] - gate_inner[:, 1])
    d_logits = jnp.where(route_hot[:, 0, :], d_first[:, None], zero_f) - jnp.where(
        route_hot[:, 1, :], d_first[:, None], zero_f
    )
    dx_piece = dx_piece.astype(jnp.bfloat16).reshape(n_section * row_total, width)
    d_logits, dx_piece = lax.optimization_barrier((d_logits, dx_piece))
    dx_red = lax.psum_scatter(dx_piece, "section", scatter_dimension=0, tiled=True)
    router_part = jnp.einsum(
        "te,tf->ef", d_logits, tokens.astype(jnp.float32), precision=highest
    )
    router_part = lax.psum(router_part, EXPERT_AXES[2])
    for name in (EXPERT_AXES[1], EXPERT_AXES[0]):
        router_part = jnp.sum(lax.all_gather(router_part, name, axis=0), axis=0)
    router_part, dx_red = lax.optimization_barrier((router_part, dx_red))
    dx_back = lax.all_to_all(dx_red.reshape(n_dev, half, LANES), EXPERT_AXES, 0, 0, tiled=True)
    dx_back = dx_back.reshape(experts, groups, half, LANES).astype(jnp.float32)
    slot_dx = jnp.sum(dx_back, axis=1).reshape(slot_total, width)
    dx_expert = jnp.dot(first_float, slot_dx, precision=highest)
    dx_expert = dx_expert + jnp.dot(second_float, slot_dx, precision=highest)
    router_float = w_router.astype(jnp.float32)
    grad_tokens = (dx_expert + jnp.dot(d_logits, router_float.T, precision=highest)).astype(
        jnp.bfloat16
    )
    grad_router = router_part.T
    return (mixed, grad_tokens, grad_router, grad_gate[None], grad_up[None], grad_down[None])


def expert_shape(devices):
    try:
        xs = sorted({d.coords[0] for d in devices.flat})
        zs = sorted({d.coords[2] for d in devices.flat})
        cores = sorted({d.core_on_chip for d in devices.flat})
        shape = (len(xs), len(zs), len(cores))
    except AttributeError:
        shape = (4, 8, 2)
    if int(np.prod(shape)) != devices.shape[1]:
        shape = (devices.shape[1] // 16, 8, 2)
    return shape


def solution(mesh):
    devices = mesh.devices
    fine = Mesh(
        devices.reshape((devices.shape[0],) + expert_shape(devices)),
        ("section",) + EXPERT_AXES,
    )
    ex = EXPERT_AXES
    in_specs = (
        P(ex, "section"),
        P(ex, "section"),
        P(ex, None),
        P("section", None),
        P(ex, None, "section"),
        P(ex, None, "section"),
        P(ex, "section", None),
    )
    out_specs = (
        P(ex, "section"),
        P(ex, "section"),
        P("section", None),
        P(ex, None, "section"),
        P(ex, None, "section"),
        P(ex, "section", None),
    )
    return jax.shard_map(
        per_device, mesh=fine, in_specs=in_specs, out_specs=out_specs, check_vma=False
    )
```

```python
import jax
import jax.numpy as jnp
import numpy as np
from jax import lax
from jax.sharding import Mesh
from jax.sharding import PartitionSpec as P

CAP = 6
LANES = 128
EXPERT_AXES = ("ex", "ez", "ec")


def expert_size():
    size = 1
    for name in EXPERT_AXES:
        size = size * lax.axis_size(name)
    return size


def per_device(tokens, cotangent, routes, w_router, w_gate, w_up, w_down):
    highest = lax.Precision.HIGHEST
    experts = w_router.shape[1]
    groups = expert_size() // experts
    capacity = CAP
    tok_count, width = tokens.shape
    n_section = lax.axis_size("section")
    slot_total = experts * capacity
    route_hot = routes[:, :, None] == jnp.arange(experts, dtype=jnp.int32)[None, None, :]
    zero_f = jnp.zeros((), jnp.float32)
    counts_flat = route_hot.astype(jnp.int32).reshape(2 * tok_count, experts)
    earlier = jnp.cumsum(counts_flat, axis=0) - counts_flat
    position = jnp.sum(earlier * counts_flat, axis=1).reshape(tok_count, 2)
    slot_row = routes * capacity + position
    slot_ids = jnp.arange(slot_total, dtype=jnp.int32)[None, :]
    pick_first = slot_row[:, 0:1] == slot_ids
    pick_second = slot_row[:, 1:2] == slot_ids
    pick_both = (pick_first | pick_second).astype(jnp.bfloat16)
    both_rows = jnp.concatenate([tokens, cotangent], axis=1)
    selected = jnp.einsum(
        "ts,td->sd", pick_both, both_rows, preferred_element_type=jnp.float32
    ).astype(jnp.bfloat16)
    zero_i = jnp.zeros((), jnp.int32)
    other_slot = jnp.sum(
        jnp.where(pick_first, routes[:, 1:2], zero_i) + jnp.where(pick_second, routes[:, 0:1], zero_i),
        axis=0,
    )
    half = capacity * width // LANES
    meta = jnp.zeros((experts, 16, LANES), jnp.bfloat16)
    meta = meta.at[:, 0, :capacity].set(other_slot.reshape(experts, capacity).astype(jnp.bfloat16))
    both_source = jnp.concatenate(
        [
            selected[:, :width].reshape(experts, half, LANES),
            selected[:, width:].reshape(experts, half, LANES),
            meta,
        ],
        axis=1,
    )
    block_rows = both_source.shape[1]
    sent = jnp.broadcast_to(
        both_source[:, None], (experts, groups, block_rows, LANES)
    ).reshape(experts * groups, block_rows, LANES)
    received = lax.all_to_all(sent, EXPERT_AXES, 0, 0, tiled=True)
    row_total = received.shape[0] * capacity
    x_recv = received[:, :half].reshape(row_total, width)
    x_rows = lax.all_gather(x_recv, "section", axis=1, tiled=True)
    cot_recv = received[:, half : 2 * half].reshape(row_total, width)
    other_recv = received[:, 2 * half, :capacity].astype(jnp.int32).reshape(row_total)
    w_router, x_recv = lax.optimization_barrier((w_router, x_recv))
    partial_logits = jnp.dot(tokens, w_router, preferred_element_type=jnp.float32)
    logits = lax.psum(partial_logits, "section")
    chosen = jnp.sum(jnp.where(route_hot, logits[:, None, :], zero_f), axis=2)
    gate_first = 1.0 / (1.0 + jnp.exp(chosen[:, 1] - chosen[:, 0]))
    gate_second = 1.0 / (1.0 + jnp.exp(chosen[:, 0] - chosen[:, 1]))
    cot_float = cotangent.astype(jnp.float32)
    row_logits = lax.psum(
        jnp.dot(x_recv, w_router, preferred_element_type=jnp.float32), "section"
    )
    own = lax.axis_index(EXPERT_AXES) // groups
    expert_ids = jnp.arange(experts, dtype=jnp.int32)[None, :]
    own_logit = jnp.sum(jnp.where(expert_ids == own, row_logits, zero_f), axis=1)
    other_logit = jnp.sum(jnp.where(expert_ids == other_recv[:, None], row_logits, zero_f), axis=1)
    row_gate = 1.0 / (1.0 + jnp.exp(other_logit - own_logit))
    row_gate, gate_first, gate_second, x_rows = lax.optimization_barrier(
        (row_gate, gate_first, gate_second, x_rows)
    )
    gate_local = w_gate[0]
    up_local = w_up[0]
    down_local = w_down[0]
    pre_gate = jnp.dot(x_rows, gate_local, preferred_element_type=jnp.float32)
    pre_up = jnp.dot(x_rows, up_local, preferred_element_type=jnp.float32)
    sigmoid_gate = jax.nn.sigmoid(pre_gate)
    activated = pre_gate * sigmoid_gate
    hidden = (activated * pre_up).astype(jnp.bfloat16)
    out_piece = jnp.dot(hidden, down_local, preferred_element_type=jnp.float32).astype(jnp.bfloat16)
    out_red = lax.psum_scatter(out_piece, "section", scatter_dimension=1, tiled=True)
    out_red, cot_recv = lax.optimization_barrier((out_red, cot_recv))
    cot_rows = lax.all_gather(cot_recv, "section", axis=1, tiled=True)
    dy_rows = (row_gate[:, None] * cot_rows.astype(jnp.float32)).astype(jnp.bfloat16)
    n_dev = row_total // capacity
    out_back = lax.all_to_all(out_red.reshape(n_dev, half, LANES), EXPERT_AXES, 0, 0, tiled=True)
    out_back = out_back.reshape(experts, groups, half, LANES).astype(jnp.float32)
    slot_out = jnp.sum(out_back, axis=1).reshape(slot_total, width)
    d_hidden = jnp.einsum("pd,fd->pf", dy_rows, down_local, preferred_element_type=jnp.float32)
    grad_down = jnp.einsum("pf,pd->fd", hidden, dy_rows, preferred_element_type=jnp.float32).astype(
        jnp.bfloat16
    )
    d_pre_gate = (
        d_hidden * pre_up * sigmoid_gate * (1.0 + pre_gate * (1.0 - sigmoid_gate))
    ).astype(jnp.bfloat16)
    d_pre_up = (d_hidden * activated).astype(jnp.bfloat16)
    grad_gate = jnp.einsum(
        "pd,pf->df", x_rows, d_pre_gate, preferred_element_type=jnp.float32
    ).astype(jnp.bfloat16)
    grad_up = jnp.einsum("pd,pf->df", x_rows, d_pre_up, preferred_element_type=jnp.float32).astype(
        jnp.bfloat16
    )
    first_float = pick_first.astype(jnp.float32)
    second_float = pick_second.astype(jnp.float32)
    out_first = jnp.dot(first_float, slot_out, precision=highest)
    out_second = jnp.dot(second_float, slot_out, precision=highest)
    mixed = (gate_first[:, None] * out_first + gate_second[:, None] * out_second).astype(
        jnp.bfloat16
    )
    local_inner = jnp.stack(
        [jnp.sum(cot_float * out_first, axis=1), jnp.sum(cot_float * out_second, axis=1)], axis=1
    )
    dx_piece = jnp.einsum("pf,df->pd", d_pre_gate, gate_local, preferred_element_type=jnp.float32)
    dx_piece = dx_piece + jnp.einsum(
        "pf,df->pd", d_pre_up, up_local, preferred_element_type=jnp.float32
    )
    gate_inner = lax.psum(local_inner, "section")
    d_first = gate_first * gate_second * (gate_inner[:, 0] - gate_inner[:, 1])
    d_logits = jnp.where(route_hot[:, 0, :], d_first[:, None], zero_f) - jnp.where(
        route_hot[:, 1, :], d_first[:, None], zero_f
    )
    dx_piece = dx_piece.astype(jnp.bfloat16)
    d_logits, dx_piece = lax.optimization_barrier((d_logits, dx_piece))
    dx_red = lax.psum_scatter(dx_piece, "section", scatter_dimension=1, tiled=True)
    router_part = jnp.einsum(
        "te,tf->ef", d_logits, tokens.astype(jnp.float32), precision=highest
    )
    router_part = lax.psum(router_part, EXPERT_AXES[2])
    for name in (EXPERT_AXES[1], EXPERT_AXES[0]):
        router_part = jnp.sum(lax.all_gather(router_part, name, axis=0), axis=0)
    router_part, dx_red = lax.optimization_barrier((router_part, dx_red))
    dx_back = lax.all_to_all(dx_red.reshape(n_dev, half, LANES), EXPERT_AXES, 0, 0, tiled=True)
    dx_back = dx_back.reshape(experts, groups, half, LANES).astype(jnp.float32)
    slot_dx = jnp.sum(dx_back, axis=1).reshape(slot_total, width)
    dx_expert = jnp.dot(first_float, slot_dx, precision=highest)
    dx_expert = dx_expert + jnp.dot(second_float, slot_dx, precision=highest)
    router_float = w_router.astype(jnp.float32)
    grad_tokens = (dx_expert + jnp.dot(d_logits, router_float.T, precision=highest)).astype(
        jnp.bfloat16
    )
    grad_router = router_part.T
    return (mixed, grad_tokens, grad_router, grad_gate[None], grad_up[None], grad_down[None])


def expert_shape(devices):
    try:
        xs = sorted({d.coords[0] for d in devices.flat})
        zs = sorted({d.coords[2] for d in devices.flat})
        cores = sorted({d.core_on_chip for d in devices.flat})
        shape = (len(xs), len(zs), len(cores))
    except AttributeError:
        shape = (4, 8, 2)
    if int(np.prod(shape)) != devices.shape[1]:
        shape = (devices.shape[1] // 16, 8, 2)
    return shape


def solution(mesh):
    devices = mesh.devices
    fine = Mesh(
        devices.reshape((devices.shape[0],) + expert_shape(devices)),
        ("section",) + EXPERT_AXES,
    )
    ex = EXPERT_AXES
    in_specs = (
        P(ex, "section"),
        P(ex, "section"),
        P(ex, None),
        P("section", None),
        P(ex, None, "section"),
        P(ex, None, "section"),
        P(ex, "section", None),
    )
    out_specs = (
        P(ex, "section"),
        P(ex, "section"),
        P("section", None),
        P(ex, None, "section"),
        P(ex, None, "section"),
        P(ex, "section", None),
    )
    return jax.shard_map(
        per_device, mesh=fine, in_specs=in_specs, out_specs=out_specs, check_vma=False
    )
```

```python
import jax
import jax.numpy as jnp
import numpy as np
from jax import lax
from jax.sharding import Mesh
from jax.sharding import PartitionSpec as P

CAP = 6
LANES = 128
EXPERT_AXES = ("ex", "ez", "ec")


def expert_size():
    size = 1
    for name in EXPERT_AXES:
        size = size * lax.axis_size(name)
    return size


def per_device(tokens, cotangent, routes, w_router, w_gate, w_up, w_down):
    highest = lax.Precision.HIGHEST
    experts = w_router.shape[1]
    groups = expert_size() // experts
    capacity = CAP
    tok_count, width = tokens.shape
    n_section = lax.axis_size("section")
    slot_total = experts * capacity
    route_hot = routes[:, :, None] == jnp.arange(experts, dtype=jnp.int32)[None, None, :]
    zero_f = jnp.zeros((), jnp.float32)
    counts_flat = route_hot.astype(jnp.int32).reshape(2 * tok_count, experts)
    earlier = jnp.cumsum(counts_flat, axis=0) - counts_flat
    position = jnp.sum(earlier * counts_flat, axis=1).reshape(tok_count, 2)
    slot_row = routes * capacity + position
    slot_ids = jnp.arange(slot_total, dtype=jnp.int32)[None, :]
    pick_first = slot_row[:, 0:1] == slot_ids
    pick_second = slot_row[:, 1:2] == slot_ids
    pick_both = (pick_first | pick_second).astype(jnp.bfloat16)
    both_rows = jnp.concatenate([tokens, cotangent], axis=1)
    selected = jnp.einsum(
        "ts,td->sd", pick_both, both_rows, preferred_element_type=jnp.float32
    ).astype(jnp.bfloat16)
    zero_i = jnp.zeros((), jnp.int32)
    other_slot = jnp.sum(
        jnp.where(pick_first, routes[:, 1:2], zero_i) + jnp.where(pick_second, routes[:, 0:1], zero_i),
        axis=0,
    )
    half = capacity * width // LANES
    meta = jnp.zeros((experts, 16, LANES), jnp.bfloat16)
    meta = meta.at[:, 0, :capacity].set(other_slot.reshape(experts, capacity).astype(jnp.bfloat16))
    def spread(block):
        rows = block.shape[1]
        return jnp.broadcast_to(block[:, None], (experts, groups, rows, LANES)).reshape(
            experts * groups, rows, LANES
        )

    x_block = selected[:, :width].reshape(experts, half, LANES)
    c_block = jnp.concatenate([selected[:, width:].reshape(experts, half, LANES), meta], axis=1)
    x_recv = lax.all_to_all(spread(x_block), EXPERT_AXES, 0, 0, tiled=True)
    row_total = x_recv.shape[0] * capacity
    x_recv = x_recv.reshape(row_total, width)
    x_rows = lax.all_gather(x_recv, "section", axis=1, tiled=True)
    c_block, x_recv = lax.optimization_barrier((c_block, x_recv))
    c_recv = lax.all_to_all(spread(c_block), EXPERT_AXES, 0, 0, tiled=True)
    cot_recv = c_recv[:, :half].reshape(row_total, width)
    other_recv = c_recv[:, half, :capacity].astype(jnp.int32).reshape(row_total)
    w_router, x_recv = lax.optimization_barrier((w_router, x_recv))
    partial_logits = jnp.dot(tokens, w_router, preferred_element_type=jnp.float32)
    logits = lax.psum(partial_logits, "section")
    chosen = jnp.sum(jnp.where(route_hot, logits[:, None, :], zero_f), axis=2)
    gate_first = 1.0 / (1.0 + jnp.exp(chosen[:, 1] - chosen[:, 0]))
    gate_second = 1.0 / (1.0 + jnp.exp(chosen[:, 0] - chosen[:, 1]))
    cot_float = cotangent.astype(jnp.float32)
    row_logits = lax.psum(
        jnp.dot(x_recv, w_router, preferred_element_type=jnp.float32), "section"
    )
    own = lax.axis_index(EXPERT_AXES) // groups
    expert_ids = jnp.arange(experts, dtype=jnp.int32)[None, :]
    own_logit = jnp.sum(jnp.where(expert_ids == own, row_logits, zero_f), axis=1)
    other_logit = jnp.sum(jnp.where(expert_ids == other_recv[:, None], row_logits, zero_f), axis=1)
    row_gate = 1.0 / (1.0 + jnp.exp(other_logit - own_logit))
    gate_local = w_gate[0]
    up_local = w_up[0]
    down_local = w_down[0]
    pre_gate = jnp.dot(x_rows, gate_local, preferred_element_type=jnp.float32)
    pre_up = jnp.dot(x_rows, up_local, preferred_element_type=jnp.float32)
    sigmoid_gate = jax.nn.sigmoid(pre_gate)
    activated = pre_gate * sigmoid_gate
    hidden = (activated * pre_up).astype(jnp.bfloat16)
    hid = gate_local.shape[1]
    down_blocks = down_local.reshape(hid, n_section, width)
    gate_blocks = gate_local.reshape(n_section, width, hid)
    up_blocks = up_local.reshape(n_section, width, hid)
    out_piece = jnp.einsum("pf,fsd->spd", hidden, down_blocks, preferred_element_type=jnp.float32)
    out_piece = out_piece.astype(jnp.bfloat16).reshape(n_section * row_total, width)
    out_red = lax.psum_scatter(out_piece, "section", scatter_dimension=0, tiled=True)
    out_red, cot_recv, row_gate, gate_first, gate_second = lax.optimization_barrier(
        (out_red, cot_recv, row_gate, gate_first, gate_second)
    )
    cot_rows = lax.all_gather(cot_recv, "section", axis=1, tiled=True)
    dy_rows = (row_gate[:, None] * cot_rows.astype(jnp.float32)).astype(jnp.bfloat16)
    n_dev = row_total // capacity
    out_back = lax.all_to_all(out_red.reshape(n_dev, half, LANES), EXPERT_AXES, 0, 0, tiled=True)
    out_back = out_back.reshape(experts, groups, half, LANES).astype(jnp.float32)
    slot_out = jnp.sum(out_back, axis=1).reshape(slot_total, width)
    d_hidden = jnp.einsum("pd,fd->pf", dy_rows, down_local, preferred_element_type=jnp.float32)
    grad_down = jnp.einsum("pf,pd->fd", hidden, dy_rows, preferred_element_type=jnp.float32).astype(
        jnp.bfloat16
    )
    d_pre_gate = (
        d_hidden * pre_up * sigmoid_gate * (1.0 + pre_gate * (1.0 - sigmoid_gate))
    ).astype(jnp.bfloat16)
    d_pre_up = (d_hidden * activated).astype(jnp.bfloat16)
    grad_gate = jnp.einsum(
        "pd,pf->df", x_rows, d_pre_gate, preferred_element_type=jnp.float32
    ).astype(jnp.bfloat16)
    grad_up = jnp.einsum("pd,pf->df", x_rows, d_pre_up, preferred_element_type=jnp.float32).astype(
        jnp.bfloat16
    )
    first_float = pick_first.astype(jnp.float32)
    second_float = pick_second.astype(jnp.float32)
    out_first = jnp.dot(first_float, slot_out, precision=highest)
    out_second = jnp.dot(second_float, slot_out, precision=highest)
    mixed = (gate_first[:, None] * out_first + gate_second[:, None] * out_second).astype(
        jnp.bfloat16
    )
    local_inner = jnp.stack(
        [jnp.sum(cot_float * out_first, axis=1), jnp.sum(cot_float * out_second, axis=1)], axis=1
    )
    dx_piece = jnp.einsum("pf,sdf->spd", d_pre_gate, gate_blocks, preferred_element_type=jnp.float32)
    dx_piece = dx_piece + jnp.einsum(
        "pf,sdf->spd", d_pre_up, up_blocks, preferred_element_type=jnp.float32
    )
    gate_inner = lax.psum(local_inner, "section")
    d_first = gate_first * gate_second * (gate_inner[:, 0] - gate_inner[:, 1])
    d_logits = jnp.where(route_hot[:, 0, :], d_first[:, None], zero_f) - jnp.where(
        route_hot[:, 1, :], d_first[:, None], zero_f
    )
    dx_piece = dx_piece.astype(jnp.bfloat16).reshape(n_section * row_total, width)
    d_logits, dx_piece = lax.optimization_barrier((d_logits, dx_piece))
    dx_red = lax.psum_scatter(dx_piece, "section", scatter_dimension=0, tiled=True)
    router_part = jnp.einsum(
        "te,tf->ef", d_logits, tokens.astype(jnp.float32), precision=highest
    )
    router_part = lax.psum(router_part, EXPERT_AXES[2])
    for name in (EXPERT_AXES[1], EXPERT_AXES[0]):
        router_part = jnp.sum(lax.all_gather(router_part, name, axis=0), axis=0)
    router_part, dx_red = lax.optimization_barrier((router_part, dx_red))
    dx_back = lax.all_to_all(dx_red.reshape(n_dev, half, LANES), EXPERT_AXES, 0, 0, tiled=True)
    dx_back = dx_back.reshape(experts, groups, half, LANES).astype(jnp.float32)
    slot_dx = jnp.sum(dx_back, axis=1).reshape(slot_total, width)
    dx_expert = jnp.dot(first_float, slot_dx, precision=highest)
    dx_expert = dx_expert + jnp.dot(second_float, slot_dx, precision=highest)
    router_float = w_router.astype(jnp.float32)
    grad_tokens = (dx_expert + jnp.dot(d_logits, router_float.T, precision=highest)).astype(
        jnp.bfloat16
    )
    grad_router = router_part.T
    return (mixed, grad_tokens, grad_router, grad_gate[None], grad_up[None], grad_down[None])


def expert_shape(devices):
    try:
        xs = sorted({d.coords[0] for d in devices.flat})
        zs = sorted({d.coords[2] for d in devices.flat})
        cores = sorted({d.core_on_chip for d in devices.flat})
        shape = (len(xs), len(zs), len(cores))
    except AttributeError:
        shape = (4, 8, 2)
    if int(np.prod(shape)) != devices.shape[1]:
        shape = (devices.shape[1] // 16, 8, 2)
    return shape


def solution(mesh):
    devices = mesh.devices
    fine = Mesh(
        devices.reshape((devices.shape[0],) + expert_shape(devices)),
        ("section",) + EXPERT_AXES,
    )
    ex = EXPERT_AXES
    in_specs = (
        P(ex, "section"),
        P(ex, "section"),
        P(ex, None),
        P("section", None),
        P(ex, None, "section"),
        P(ex, None, "section"),
        P(ex, "section", None),
    )
    out_specs = (
        P(ex, "section"),
        P(ex, "section"),
        P("section", None),
        P(ex, None, "section"),
        P(ex, None, "section"),
        P(ex, "section", None),
    )
    return jax.shard_map(
        per_device, mesh=fine, in_specs=in_specs, out_specs=out_specs, check_vma=False
    )
```

```python
import jax
import jax.numpy as jnp
import numpy as np
from jax import lax
from jax.sharding import Mesh
from jax.sharding import PartitionSpec as P

CAP = 6
LANES = 128
EXPERT_AXES = ("ex", "ez", "ec")


def expert_size():
    size = 1
    for name in EXPERT_AXES:
        size = size * lax.axis_size(name)
    return size


def per_device(tokens, cotangent, routes, w_router, w_gate, w_up, w_down):
    highest = lax.Precision.HIGHEST
    experts = w_router.shape[1]
    groups = expert_size() // experts
    capacity = CAP
    tok_count, width = tokens.shape
    n_section = lax.axis_size("section")
    slot_total = experts * capacity
    route_hot = routes[:, :, None] == jnp.arange(experts, dtype=jnp.int32)[None, None, :]
    zero_f = jnp.zeros((), jnp.float32)
    counts_flat = route_hot.astype(jnp.int32).reshape(2 * tok_count, experts)
    earlier = jnp.cumsum(counts_flat, axis=0) - counts_flat
    position = jnp.sum(earlier * counts_flat, axis=1).reshape(tok_count, 2)
    slot_row = routes * capacity + position
    slot_ids = jnp.arange(slot_total, dtype=jnp.int32)[None, :]
    pick_first = slot_row[:, 0:1] == slot_ids
    pick_second = slot_row[:, 1:2] == slot_ids
    pick_both = (pick_first | pick_second).astype(jnp.bfloat16)
    x_source = jnp.einsum(
        "ts,td->sd", pick_both, tokens, preferred_element_type=jnp.float32
    ).astype(jnp.bfloat16)
    zero_i = jnp.zeros((), jnp.int32)
    other_slot = jnp.sum(
        jnp.where(pick_first, routes[:, 1:2], zero_i) + jnp.where(pick_second, routes[:, 0:1], zero_i),
        axis=0,
    )
    half = capacity * width // LANES
    meta = jnp.zeros((experts, 16, LANES), jnp.bfloat16)
    meta = meta.at[:, 0, :capacity].set(other_slot.reshape(experts, capacity).astype(jnp.bfloat16))
    def spread(block):
        rows = block.shape[1]
        return jnp.broadcast_to(block[:, None], (experts, groups, rows, LANES)).reshape(
            experts * groups, rows, LANES
        )

    x_block = x_source.reshape(experts, half, LANES)
    x_recv = lax.all_to_all(spread(x_block), EXPERT_AXES, 0, 0, tiled=True)
    cot_source = jnp.einsum(
        "ts,td->sd", pick_both, cotangent, preferred_element_type=jnp.float32
    ).astype(jnp.bfloat16)
    c_block = jnp.concatenate([cot_source.reshape(experts, half, LANES), meta], axis=1)
    row_total = x_recv.shape[0] * capacity
    x_recv = x_recv.reshape(row_total, width)
    x_rows = lax.all_gather(x_recv, "section", axis=1, tiled=True)
    c_block, x_recv = lax.optimization_barrier((c_block, x_recv))
    c_recv = lax.all_to_all(spread(c_block), EXPERT_AXES, 0, 0, tiled=True)
    cot_recv = c_recv[:, :half].reshape(row_total, width)
    other_recv = c_recv[:, half, :capacity].astype(jnp.int32).reshape(row_total)
    w_router, x_recv = lax.optimization_barrier((w_router, x_recv))
    partial_logits = jnp.dot(tokens, w_router, preferred_element_type=jnp.float32)
    logits = lax.psum(partial_logits, "section")
    chosen = jnp.sum(jnp.where(route_hot, logits[:, None, :], zero_f), axis=2)
    gate_first = 1.0 / (1.0 + jnp.exp(chosen[:, 1] - chosen[:, 0]))
    gate_second = 1.0 / (1.0 + jnp.exp(chosen[:, 0] - chosen[:, 1]))
    cot_float = cotangent.astype(jnp.float32)
    row_logits = lax.psum(
        jnp.dot(x_recv, w_router, preferred_element_type=jnp.float32), "section"
    )
    own = lax.axis_index(EXPERT_AXES) // groups
    expert_ids = jnp.arange(experts, dtype=jnp.int32)[None, :]
    own_logit = jnp.sum(jnp.where(expert_ids == own, row_logits, zero_f), axis=1)
    other_logit = jnp.sum(jnp.where(expert_ids == other_recv[:, None], row_logits, zero_f), axis=1)
    row_gate = 1.0 / (1.0 + jnp.exp(other_logit - own_logit))
    gate_local = w_gate[0]
    up_local = w_up[0]
    down_local = w_down[0]
    pre_gate = jnp.dot(x_rows, gate_local, preferred_element_type=jnp.float32)
    pre_up = jnp.dot(x_rows, up_local, preferred_element_type=jnp.float32)
    sigmoid_gate = jax.nn.sigmoid(pre_gate)
    activated = pre_gate * sigmoid_gate
    hidden = (activated * pre_up).astype(jnp.bfloat16)
    hid = gate_local.shape[1]
    down_blocks = down_local.reshape(hid, n_section, width)
    gate_blocks = gate_local.reshape(n_section, width, hid)
    up_blocks = up_local.reshape(n_section, width, hid)
    out_piece = jnp.einsum("pf,fsd->spd", hidden, down_blocks, preferred_element_type=jnp.float32)
    out_piece = out_piece.astype(jnp.bfloat16).reshape(n_section * row_total, width)
    out_red = lax.psum_scatter(out_piece, "section", scatter_dimension=0, tiled=True)
    out_red, cot_recv, row_gate, gate_first, gate_second = lax.optimization_barrier(
        (out_red, cot_recv, row_gate, gate_first, gate_second)
    )
    cot_rows = lax.all_gather(cot_recv, "section", axis=1, tiled=True)
    dy_rows = (row_gate[:, None] * cot_rows.astype(jnp.float32)).astype(jnp.bfloat16)
    n_dev = row_total // capacity
    out_back = lax.all_to_all(out_red.reshape(n_dev, half, LANES), EXPERT_AXES, 0, 0, tiled=True)
    out_back = out_back.reshape(experts, groups, half, LANES).astype(jnp.float32)
    slot_out = jnp.sum(out_back, axis=1).reshape(slot_total, width)
    d_hidden = jnp.einsum("pd,fd->pf", dy_rows, down_local, preferred_element_type=jnp.float32)
    grad_down = jnp.einsum("pf,pd->fd", hidden, dy_rows, preferred_element_type=jnp.float32).astype(
        jnp.bfloat16
    )
    d_pre_gate = (
        d_hidden * pre_up * sigmoid_gate * (1.0 + pre_gate * (1.0 - sigmoid_gate))
    ).astype(jnp.bfloat16)
    d_pre_up = (d_hidden * activated).astype(jnp.bfloat16)
    grad_gate = jnp.einsum(
        "pd,pf->df", x_rows, d_pre_gate, preferred_element_type=jnp.float32
    ).astype(jnp.bfloat16)
    grad_up = jnp.einsum("pd,pf->df", x_rows, d_pre_up, preferred_element_type=jnp.float32).astype(
        jnp.bfloat16
    )
    first_float = pick_first.astype(jnp.float32)
    second_float = pick_second.astype(jnp.float32)
    out_first = jnp.dot(first_float, slot_out, precision=highest)
    out_second = jnp.dot(second_float, slot_out, precision=highest)
    mixed = (gate_first[:, None] * out_first + gate_second[:, None] * out_second).astype(
        jnp.bfloat16
    )
    local_inner = jnp.stack(
        [jnp.sum(cot_float * out_first, axis=1), jnp.sum(cot_float * out_second, axis=1)], axis=1
    )
    dx_piece = jnp.einsum("pf,sdf->spd", d_pre_gate, gate_blocks, preferred_element_type=jnp.float32)
    dx_piece = dx_piece + jnp.einsum(
        "pf,sdf->spd", d_pre_up, up_blocks, preferred_element_type=jnp.float32
    )
    gate_inner = lax.psum(local_inner, "section")
    d_first = gate_first * gate_second * (gate_inner[:, 0] - gate_inner[:, 1])
    d_logits = jnp.where(route_hot[:, 0, :], d_first[:, None], zero_f) - jnp.where(
        route_hot[:, 1, :], d_first[:, None], zero_f
    )
    dx_piece = dx_piece.astype(jnp.bfloat16).reshape(n_section * row_total, width)
    d_logits, dx_piece = lax.optimization_barrier((d_logits, dx_piece))
    dx_red = lax.psum_scatter(dx_piece, "section", scatter_dimension=0, tiled=True)
    router_part = jnp.einsum(
        "te,tf->ef", d_logits, tokens.astype(jnp.float32), precision=highest
    )
    router_part = lax.psum(router_part, EXPERT_AXES[2])
    for name in (EXPERT_AXES[1], EXPERT_AXES[0]):
        router_part = jnp.sum(lax.all_gather(router_part, name, axis=0), axis=0)
    router_part, dx_red = lax.optimization_barrier((router_part, dx_red))
    dx_back = lax.all_to_all(dx_red.reshape(n_dev, half, LANES), EXPERT_AXES, 0, 0, tiled=True)
    dx_back = dx_back.reshape(experts, groups, half, LANES).astype(jnp.float32)
    slot_dx = jnp.sum(dx_back, axis=1).reshape(slot_total, width)
    dx_expert = jnp.dot(first_float, slot_dx, precision=highest)
    dx_expert = dx_expert + jnp.dot(second_float, slot_dx, precision=highest)
    router_float = w_router.astype(jnp.float32)
    grad_tokens = (dx_expert + jnp.dot(d_logits, router_float.T, precision=highest)).astype(
        jnp.bfloat16
    )
    grad_router = router_part.T
    return (mixed, grad_tokens, grad_router, grad_gate[None], grad_up[None], grad_down[None])


def expert_shape(devices):
    try:
        xs = sorted({d.coords[0] for d in devices.flat})
        zs = sorted({d.coords[2] for d in devices.flat})
        cores = sorted({d.core_on_chip for d in devices.flat})
        shape = (len(xs), len(zs), len(cores))
    except AttributeError:
        shape = (4, 8, 2)
    if int(np.prod(shape)) != devices.shape[1]:
        shape = (devices.shape[1] // 16, 8, 2)
    return shape


def solution(mesh):
    devices = mesh.devices
    fine = Mesh(
        devices.reshape((devices.shape[0],) + expert_shape(devices)),
        ("section",) + EXPERT_AXES,
    )
    ex = EXPERT_AXES
    in_specs = (
        P(ex, "section"),
        P(ex, "section"),
        P(ex, None),
        P("section", None),
        P(ex, None, "section"),
        P(ex, None, "section"),
        P(ex, "section", None),
    )
    out_specs = (
        P(ex, "section"),
        P(ex, "section"),
        P("section", None),
        P(ex, None, "section"),
        P(ex, None, "section"),
        P(ex, "section", None),
    )
    return jax.shard_map(
        per_device, mesh=fine, in_specs=in_specs, out_specs=out_specs, check_vma=False
    )
```
